32 devices in a mesh: groups: 2 (over x), ctx: 16 (over z, y, core).
Axes of the slice: x: 2, y: 2, z: 4, core: 2. Of those that a mesh axis runs over, the one named last changes fastest.
Arguments:
- tokens: bfloat16 [8192, 2048], P(('groups', 'ctx')), parts along dimension 0, may hold values from -6 to 6
- kernel: float32 [3, 2048], replicated, may hold values from -3 to 3
- w_query: bfloat16 [2048, 256], P('ctx'), may hold values from -0.125 to 0.125
- w_key: bfloat16 [2048, 256], P('ctx'), may hold values from -0.125 to 0.125
- w_value: bfloat16 [2048, 1024], P('ctx'), may hold values from -0.125 to 0.125
- cotangent: bfloat16 [8192, 1024], P(('groups', 'ctx')), parts along dimension 0, may hold values from -6 to 6
Outputs:
- mixed: bfloat16 [8192, 1024], P(('groups', 'ctx')), parts along dimension 0
- grad_tokens: bfloat16 [8192, 2048], P(('groups', 'ctx')), parts along dimension 0
- grad_query: float32 [4096, 256], P(('groups', 'ctx')), parts along dimension 0
- grad_key: float32 [4096, 256], P(('groups', 'ctx')), parts along dimension 0
- grad_value: float32 [4096, 1024], P(('groups', 'ctx')), parts along dimension 0
- grad_kernel: float32 [6, 2048], P('groups', 'ctx'), parts along dimension 0
The draws below stay inside these ranges and needn't reach their ends.
There are 2 independent parts, one for each index of `groups`. The reference program is written for one: setup_inputs(seed, part) draws one part's arguments, and reference() takes and returns one part's arrays. A program takes and returns all parts, laid end to end along the dimension named above; an argument that names none is the same for every part. Nothing has to cross between parts.
All inputs are finite; a program needn't handle non-finite values.
Results may differ from the reference program's by a relative error of at most 0.009.
Values may be sent and summed in bfloat16 or wider, within the bound.
No kernel may reach another device: no remote copies, remote signals or barrier semaphores. Data moves between devices by JAX's collectives and lax.ppermute only.
A program may use at most 128 MiB of HBM per device.

```python
import jax
import jax.numpy as jnp
import numpy as np
from jax import lax

D = 2048
HEADS = 16
FEAT = 16
HEAD_DIM = 64
TOK_DEV = 256
SEQ = 4096
N_CTX = 16


def spiked(drawn, own_key, source, target, parts, factor):
    def block_of(axis_at):
        return (jnp.arange(drawn.shape[axis_at]) // (drawn.shape[axis_at] // parts)).reshape((-1,) + (1,) * (drawn.ndim - 1 - axis_at))

    one_side = jax.random.permutation(own_key, parts)[block_of(target)]
    second = (block_of(target) + parts // 2) % parts
    return jnp.where((block_of(source) == one_side) | (block_of(source) == second), factor * drawn, drawn)


def block_levels(own_key, shape, split, low, largest):
    factor_of = 1.0
    for axis_at, shards_of in split:
        heights = jax.random.uniform(jax.random.fold_in(jax.random.fold_in(own_key, 6), axis_at), (shards_of,), jnp.float32, low / len(split), largest / len(split))
        factor_of = factor_of * jnp.repeat(jnp.exp(heights), shape[axis_at] // shards_of).reshape((-1,) + (1,) * (len(shape) - 1 - axis_at))
    return factor_of


def centred(own_key, dims, scale, reach, pieces=(), dtype=jnp.bfloat16):
    result = jax.random.normal(own_key, dims, jnp.float32) * scale
    if len(pieces) > 0:
        result = block_levels(own_key, dims, pieces, -0.22, 0.18) * result
    return jnp.clip(result, min=-reach, max=reach).astype(dtype)


def heavy_noise(own_key, dims, spread, bound, shards, heavy, dtype=jnp.bfloat16):
    entries = spread * jax.random.normal(own_key, dims, jnp.float32)
    if shards:
        entries = entries * block_levels(own_key, dims, shards, -0.22, 0.18)
    return jnp.clip(spiked(entries, jax.random.fold_in(own_key, 3), *heavy), -bound, bound).astype(dtype)


def setup_inputs(seed: int = 0, part: int = 0) -> dict:
    key_list = jax.random.split(jax.random.key(seed), 7)
    part_keys = jax.random.split(jax.random.fold_in(key_list[6], part), 7)
    tokens = heavy_noise(part_keys[0], (SEQ, D), 1.0, 6.0, ((0, 16),), (0, 1, 16, 2.0))
    kernel = centred(key_list[1], (3, D), 0.5, 3.0, (), jnp.float32)
    w_query = centred(key_list[2], (D, HEADS * FEAT), D ** -0.5, 0.125, ((0, 16),))
    w_key = centred(key_list[3], (D, HEADS * FEAT), D ** -0.5, 0.125, ((0, 16),))
    w_value = centred(key_list[4], (D, HEADS * HEAD_DIM), D ** -0.5, 0.125, ((0, 16),))
    cotangent = centred(part_keys[5], (SEQ, HEADS * HEAD_DIM), 1.0, 6.0, ((0, 16),))
    return {"tokens": tokens, "kernel": kernel, "w_query": w_query, "w_key": w_key, "w_value": w_value, "cotangent": cotangent}


def pair_tables(feat):
    rows, cols = np.triu_indices(feat)
    coef = np.where(rows == cols, 1.0 / np.sqrt(2.0 * feat), 1.0 / np.sqrt(1.0 * feat))
    return (rows, cols, coef)

def features(block):
    feat = block.shape[-1]
    rows, cols, coef = pair_tables(feat)
    scale = jnp.asarray(coef, jnp.float32)
    quad = block[..., rows] * block[..., cols] * scale
    ones = jnp.ones(block.shape[:-1] + (1,), jnp.float32)
    return jnp.concatenate((ones, block * feat ** (-0.25), quad), axis=-1)

def block_attend(query, key, value, state, norm):
    length, heads, feat = query.shape
    hdim = value.shape[2]
    width = state.shape[0]
    high = lax.Precision.HIGHEST
    sigma = jnp.einsum('thf,shf->hts', query, key, precision=high) / np.sqrt(1.0 * feat)
    weight = 1.0 + sigma + 0.5 * sigma * sigma
    causal = lax.broadcasted_iota(jnp.int32, (length, length), 0) >= lax.broadcasted_iota(jnp.int32, (length, length), 1)
    weight = jnp.where(causal[None], weight, jnp.float32(0.0))
    numer = jnp.einsum('hts,she->the', weight, value, precision=high)
    denom = lax.optimization_barrier(jnp.sum(weight, axis=2)).T
    phi_query = features(query)
    numer = numer + jnp.einsum('thn,nhe->the', phi_query, state.reshape(width, heads, hdim), precision=high)
    denom = denom + jnp.einsum('thn,nh->th', phi_query, norm, precision=high)
    attended = numer / denom[:, :, None]
    scaled = attended * lax.rsqrt(lax.optimization_barrier(jnp.mean(attended * attended, axis=2, keepdims=True)) + 1e-06)
    return scaled.reshape(length, heads * hdim)

def block_state(key, value):
    length, heads, hdim = value.shape
    phi_key = features(key)
    state = jnp.einsum('shn,she->nhe', phi_key, value, precision=lax.Precision.HIGHEST)
    return (state.reshape(phi_key.shape[2], heads * hdim), lax.optimization_barrier(jnp.sum(phi_key, axis=0)).T)

def attention(query, key, value):
    width = 1 + FEAT + FEAT * (FEAT + 1) // 2
    qb = query.reshape(N_CTX, TOK_DEV, HEADS, FEAT)
    kb = key.reshape(N_CTX, TOK_DEV, HEADS, FEAT)
    vb = value.reshape(N_CTX, TOK_DEV, HEADS, HEAD_DIM)

    def step(carry, blocks):
        state, norm = carry
        qi, ki, vi = blocks
        out = block_attend(qi, ki, vi, state, norm)
        own_state, own_norm = block_state(ki, vi)
        return ((state + own_state, norm + own_norm), out)
    start = (jnp.zeros((width, HEADS * HEAD_DIM), jnp.float32), jnp.zeros((width, HEADS), jnp.float32))
    _, outs = lax.scan(step, start, (qb, kb, vb))
    return outs.reshape(N_CTX * TOK_DEV, HEADS * HEAD_DIM)

def conv_gate(tokens_f, kernel):
    padded = jnp.concatenate((jnp.zeros((2, tokens_f.shape[1]), jnp.float32), tokens_f), axis=0)
    conv = kernel[0] * padded[2:] + kernel[1] * padded[1:-1] + kernel[2] * padded[:-2]
    return tokens_f + jax.nn.sigmoid(tokens_f) * conv

def reference(tokens, kernel, w_query, w_key, w_value, cotangent):
    total = tokens.shape[0]
    tokens_f = tokens.astype(jnp.float32)
    gated = conv_gate(tokens_f, kernel).astype(jnp.bfloat16)
    query = jnp.dot(gated, w_query, preferred_element_type=jnp.float32).astype(jnp.bfloat16)
    key = jnp.dot(gated, w_key, preferred_element_type=jnp.float32).astype(jnp.bfloat16)
    value = jnp.dot(gated, w_value, preferred_element_type=jnp.float32).astype(jnp.bfloat16)
    query_f = query.astype(jnp.float32).reshape(total, HEADS, FEAT)
    key_f = key.astype(jnp.float32).reshape(total, HEADS, FEAT)
    value_f = value.astype(jnp.float32).reshape(total, HEADS, HEAD_DIM)
    out_f, back = jax.vjp(attention, query_f, key_f, value_f)
    mixed = out_f.astype(jnp.bfloat16)
    d_query, d_key, d_value = back(cotangent.astype(jnp.float32))
    d_query = d_query.reshape(total, HEADS * FEAT).astype(jnp.bfloat16)
    d_key = d_key.reshape(total, HEADS * FEAT).astype(jnp.bfloat16)
    d_value = d_value.reshape(total, HEADS * HEAD_DIM).astype(jnp.bfloat16)
    d_gated = jnp.dot(d_query, w_query.T, preferred_element_type=jnp.float32)
    d_gated = d_gated + jnp.dot(d_key, w_key.T, preferred_element_type=jnp.float32)
    d_gated = d_gated + jnp.dot(d_value, w_value.T, preferred_element_type=jnp.float32)
    grad_query = jnp.dot(gated.T, d_query, preferred_element_type=jnp.float32)
    grad_key = jnp.dot(gated.T, d_key, preferred_element_type=jnp.float32)
    grad_value = jnp.dot(gated.T, d_value, preferred_element_type=jnp.float32)
    _, back_conv = jax.vjp(conv_gate, tokens_f, kernel)
    grad_tokens, grad_kernel = back_conv(d_gated)
    return (mixed, grad_tokens.astype(jnp.bfloat16), grad_query, grad_key, grad_value, grad_kernel)
```

```python
import jax
import jax.numpy as jnp
import numpy as np
from jax import lax
from jax.sharding import Mesh
from jax.sharding import PartitionSpec as P

HEADS = 16
FEAT = 16
HEAD_DIM = 64


def from_behind(value, axis, steps):
    count = lax.axis_size(axis)
    first, last = (max(0, -steps), min(count, count - steps))
    return lax.ppermute(value, axis, [(source, source + steps) for source in range(first, last)])


def pair_tables(feat):
    rows, cols = np.triu_indices(feat)
    coef = np.where(rows == cols, 1.0 / np.sqrt(2.0 * feat), 1.0 / np.sqrt(1.0 * feat))
    return (rows, cols, coef)


def features(block):
    feat = block.shape[-1]
    rows, cols, coef = pair_tables(feat)
    scale = jnp.asarray(coef, jnp.float32)
    eye = np.eye(feat, dtype=np.float32)
    high = lax.Precision.HIGHEST
    pick_rows = jnp.einsum("...f,fp->...p", block, jnp.asarray(eye[:, rows]), precision=high)
    pick_cols = jnp.einsum("...f,fp->...p", block, jnp.asarray(eye[:, cols]), precision=high)
    quad = pick_rows * pick_cols * scale
    ones = jnp.ones(block.shape[:-1] + (1,), jnp.float32)
    return jnp.concatenate((ones, block * feat ** (-0.25), quad), axis=-1)


def block_attend(query, key, value, state, norm):
    length, heads, feat = query.shape
    hdim = value.shape[2]
    width = state.shape[0]
    high = lax.Precision.HIGHEST
    sigma = jnp.einsum("thf,shf->hts", query, key, precision=high) / np.sqrt(1.0 * feat)
    weight = 1.0 + sigma + 0.5 * sigma * sigma
    causal = lax.broadcasted_iota(jnp.int32, (length, length), 0) >= lax.broadcasted_iota(
        jnp.int32, (length, length), 1
    )
    weight = jnp.where(causal[None], weight, jnp.float32(0.0))
    numer = jnp.einsum("hts,she->the", weight, value, precision=high)
    denom = jnp.sum(weight, axis=2).T
    phi_query = features(query)
    numer = numer + jnp.einsum(
        "thn,nhe->the", phi_query, state.reshape(width, heads, hdim), precision=high
    )
    denom = denom + jnp.einsum("thn,nh->th", phi_query, norm, precision=high)
    attended = numer / denom[:, :, None]
    scaled = attended * lax.rsqrt(jnp.mean(attended * attended, axis=2, keepdims=True) + 1e-06)
    return scaled.reshape(length, heads * hdim)


def block_state(key, value):
    length, heads, hdim = value.shape
    phi_key = features(key)
    state = jnp.einsum("shn,she->nhe", phi_key, value, precision=lax.Precision.HIGHEST)
    return (state.reshape(phi_key.shape[2], heads * hdim), jnp.sum(phi_key, axis=0).T)


def pack_parts(state, norm, devices):
    flat = jnp.concatenate((state.reshape(-1), norm.reshape(-1)), axis=0)
    total = flat.shape[0]
    piece = -(-total // (devices * 128)) * 128
    flat = jnp.concatenate((flat, jnp.zeros((devices * piece - total,), jnp.float32)), axis=0)
    return flat.reshape(devices, piece)


def unpack_parts(parts, state, norm):
    flat = parts.reshape(-1)
    count = state.size
    new_state = flat[:count].reshape(state.shape)
    new_norm = flat[count : count + norm.size].reshape(norm.shape)
    return (new_state, new_norm)


def before_sum(block):
    zero_row = jnp.zeros((1, block.shape[1]), jnp.float32)
    return jnp.concatenate((zero_row, jnp.cumsum(block, axis=0)[:-1]), axis=0)


def after_sum(block):
    zero_row = jnp.zeros((1, block.shape[1]), jnp.float32)
    return jnp.concatenate((lax.cumsum(block[1:], axis=0, reverse=True), zero_row), axis=0)


def local_gate(tokens_f, rim_f, kernel):
    padded = jnp.concatenate((rim_f, tokens_f), axis=0)
    conv = kernel[0] * padded[2:] + kernel[1] * padded[1:-1] + kernel[2] * padded[:-2]
    return tokens_f + jax.nn.sigmoid(tokens_f) * conv


CTX = ("chip", "core")


def to_split_order(block, chips, rows):
    length = block.shape[0]
    return block.reshape(length, chips, 2, rows).transpose(0, 2, 1, 3).reshape(length, -1)


def from_split_order(block, chips, rows):
    length = block.shape[0]
    return block.reshape(length, 2, chips, rows).transpose(0, 2, 1, 3).reshape(length, -1)


def gather_rows(block):
    part = lax.all_gather(block, "chip", axis=0, tiled=True)
    return lax.all_gather(part, "core", axis=0, tiled=True)


def scatter_rows(block):
    part = lax.psum_scatter(block, "core", scatter_dimension=0, tiled=True)
    return lax.psum_scatter(part, "chip", scatter_dimension=0, tiled=True)


def body(tokens, kernel, w_query, w_key, w_value, cotangent):
    length = tokens.shape[0]
    qk_cols = w_query.shape[1]
    chips = lax.axis_size("chip")
    devices = chips * lax.axis_size("core")
    rows = w_query.shape[0]
    rim = from_behind(tokens[length - 2 :], CTX, 1)
    tokens_f = tokens.astype(jnp.float32)
    rim_f = rim.astype(jnp.float32)
    gated = local_gate(tokens_f, rim_f, kernel).astype(jnp.bfloat16)
    stacked = jnp.concatenate((w_query, w_key, w_value), axis=1)
    full = gather_rows(stacked)
    columns = to_split_order(gated, chips, rows)
    projected = jnp.dot(columns, full, preferred_element_type=jnp.float32)
    projected = projected.astype(jnp.bfloat16)
    query_f = projected[:, :qk_cols].astype(jnp.float32).reshape(length, HEADS, FEAT)
    key_f = projected[:, qk_cols : 2 * qk_cols].astype(jnp.float32).reshape(length, HEADS, FEAT)
    value_f = projected[:, 2 * qk_cols :].astype(jnp.float32).reshape(length, HEADS, HEAD_DIM)
    own_state, own_norm = block_state(key_f, value_f)
    state_blocks = pack_parts(own_state, own_norm, devices)
    prefix_parts = before_sum(
        lax.all_to_all(state_blocks, CTX, split_axis=0, concat_axis=0, tiled=True)
    )
    prefix_home = lax.all_to_all(prefix_parts, CTX, split_axis=0, concat_axis=0, tiled=True)
    prev_state, prev_norm = unpack_parts(prefix_home, own_state, own_norm)
    out_f, back = jax.vjp(block_attend, query_f, key_f, value_f, prev_state, prev_norm)
    mixed = out_f.astype(jnp.bfloat16)
    d_query, d_key, d_value, d_state, d_norm = back(cotangent.astype(jnp.float32))
    grad_blocks = pack_parts(d_state, d_norm, devices)
    suffix_parts = after_sum(
        lax.all_to_all(grad_blocks, CTX, split_axis=0, concat_axis=0, tiled=True)
    )
    suffix_home = lax.all_to_all(suffix_parts, CTX, split_axis=0, concat_axis=0, tiled=True)
    later_state, later_norm = unpack_parts(suffix_home, d_state, d_norm)
    _, back_state = jax.vjp(block_state, key_f, value_f)
    extra_key, extra_value = back_state((later_state, later_norm))
    d_proj = jnp.concatenate(
        (
            d_query.reshape(length, qk_cols),
            (d_key + extra_key).reshape(length, qk_cols),
            (d_value + extra_value).reshape(length, HEADS * HEAD_DIM),
        ),
        axis=1,
    ).astype(jnp.bfloat16)
    d_gated = lax.dot_general(
        d_proj, full, (((1,), (1,)), ((), ())), preferred_element_type=jnp.float32
    )
    d_gated = from_split_order(d_gated, chips, rows)
    grads = scatter_rows(
        lax.dot_general(
            columns, d_proj, (((0,), (0,)), ((), ())), preferred_element_type=jnp.float32
        )
    )
    _, back_conv = jax.vjp(local_gate, tokens_f, rim_f, kernel)
    d_tokens, d_rim, d_kernel = back_conv(d_gated)
    carried = from_behind(d_rim, CTX, -1)
    d_tokens = jnp.concatenate((d_tokens[: length - 2], d_tokens[length - 2 :] + carried), axis=0)
    kernel_share = lax.psum_scatter(d_kernel, CTX, scatter_dimension=1, tiled=True)
    return (
        mixed,
        d_tokens.astype(jnp.bfloat16),
        grads[:, :qk_cols],
        grads[:, qk_cols : 2 * qk_cols],
        grads[:, 2 * qk_cols :],
        kernel_share,
    )


def solution(mesh):
    groups, ctx = mesh.devices.shape
    split = Mesh(mesh.devices.reshape(groups, ctx // 2, 2), ("groups",) + CTX)
    rows_all = ("groups",) + CTX
    in_specs = (
        P(rows_all, None),
        P(),
        P(CTX, None),
        P(CTX, None),
        P(CTX, None),
        P(rows_all, None),
    )
    out_specs = (
        P(rows_all, None),
        P(rows_all, None),
        P(rows_all, None),
        P(rows_all, None),
        P(rows_all, None),
        P("groups", CTX),
    )
    return jax.shard_map(body, mesh=split, in_specs=in_specs, out_specs=out_specs, check_vma=False)
```

```python
import jax
import jax.numpy as jnp
import numpy as np
from jax import lax
from jax.sharding import PartitionSpec as P

HEADS = 16
FEAT = 16
HEAD_DIM = 64


def from_behind(value, axis, steps):
    count = lax.axis_size(axis)
    first, last = (max(0, -steps), min(count, count - steps))
    return lax.ppermute(value, axis, [(source, source + steps) for source in range(first, last)])


def pair_tables(feat):
    rows, cols = np.triu_indices(feat)
    coef = np.where(rows == cols, 1.0 / np.sqrt(2.0 * feat), 1.0 / np.sqrt(1.0 * feat))
    return (rows, cols, coef)


def features(block):
    feat = block.shape[-1]
    rows, cols, coef = pair_tables(feat)
    scale = jnp.asarray(coef, jnp.float32)
    eye = np.eye(feat, dtype=np.float32)
    high = lax.Precision.HIGHEST
    pick_rows = jnp.einsum("...f,fp->...p", block, jnp.asarray(eye[:, rows]), precision=high)
    pick_cols = jnp.einsum("...f,fp->...p", block, jnp.asarray(eye[:, cols]), precision=high)
    quad = pick_rows * pick_cols * scale
    ones = jnp.ones(block.shape[:-1] + (1,), jnp.float32)
    return jnp.concatenate((ones, block * feat ** (-0.25), quad), axis=-1)


def block_attend(query, key, value, state, norm):
    length, heads, feat = query.shape
    hdim = value.shape[2]
    width = state.shape[0]
    high = lax.Precision.HIGHEST
    sigma = jnp.einsum("thf,shf->hts", query, key, precision=high) / np.sqrt(1.0 * feat)
    weight = 1.0 + sigma + 0.5 * sigma * sigma
    causal = lax.broadcasted_iota(jnp.int32, (length, length), 0) >= lax.broadcasted_iota(
        jnp.int32, (length, length), 1
    )
    weight = jnp.where(causal[None], weight, jnp.float32(0.0))
    numer = jnp.einsum("hts,she->the", weight, value, precision=high)
    denom = jnp.sum(weight, axis=2).T
    phi_query = features(query)
    numer = numer + jnp.einsum(
        "thn,nhe->the", phi_query, state.reshape(width, heads, hdim), precision=high
    )
    denom = denom + jnp.einsum("thn,nh->th", phi_query, norm, precision=high)
    attended = numer / denom[:, :, None]
    scaled = attended * lax.rsqrt(jnp.mean(attended * attended, axis=2, keepdims=True) + 1e-06)
    return scaled.reshape(length, heads * hdim)


def block_state(key, value):
    length, heads, hdim = value.shape
    phi_key = features(key)
    state = jnp.einsum("shn,she->nhe", phi_key, value, precision=lax.Precision.HIGHEST)
    return (state.reshape(phi_key.shape[2], heads * hdim), jnp.sum(phi_key, axis=0).T)


def pack_parts(state, norm, devices):
    flat = jnp.concatenate((state.reshape(-1), norm.reshape(-1)), axis=0)
    total = flat.shape[0]
    piece = -(-total // (devices * 128)) * 128
    flat = jnp.concatenate((flat, jnp.zeros((devices * piece - total,), jnp.float32)), axis=0)
    return flat.reshape(devices, piece)


def unpack_parts(parts, state, norm):
    flat = parts.reshape(-1)
    count = state.size
    new_state = flat[:count].reshape(state.shape)
    new_norm = flat[count : count + norm.size].reshape(norm.shape)
    return (new_state, new_norm)


def before_sum(block):
    zero_row = jnp.zeros((1, block.shape[1]), jnp.float32)
    return jnp.concatenate((zero_row, jnp.cumsum(block, axis=0)[:-1]), axis=0)


def after_sum(block):
    zero_row = jnp.zeros((1, block.shape[1]), jnp.float32)
    return jnp.concatenate((lax.cumsum(block[1:], axis=0, reverse=True), zero_row), axis=0)


def local_gate(tokens_f, rim_f, kernel):
    padded = jnp.concatenate((rim_f, tokens_f), axis=0)
    conv = kernel[0] * padded[2:] + kernel[1] * padded[1:-1] + kernel[2] * padded[:-2]
    return tokens_f + jax.nn.sigmoid(tokens_f) * conv


def body(tokens, kernel, w_query, w_key, w_value, cotangent):
    length = tokens.shape[0]
    qk_cols = w_query.shape[1]
    devices = lax.axis_size("ctx")
    rim = from_behind(tokens[length - 2 :], "ctx", 1)
    tokens_f = tokens.astype(jnp.float32)
    rim_f = rim.astype(jnp.float32)
    gated = local_gate(tokens_f, rim_f, kernel).astype(jnp.bfloat16)
    full_qk = lax.all_gather(jnp.concatenate((w_query, w_key), axis=1), "ctx", axis=0, tiled=True)
    full_v = lax.all_gather(w_value, "ctx", axis=0, tiled=True)
    proj_qk = jnp.dot(gated, full_qk, preferred_element_type=jnp.float32).astype(jnp.bfloat16)
    proj_v = jnp.dot(gated, full_v, preferred_element_type=jnp.float32).astype(jnp.bfloat16)
    query_f = proj_qk[:, :qk_cols].astype(jnp.float32).reshape(length, HEADS, FEAT)
    key_f = proj_qk[:, qk_cols:].astype(jnp.float32).reshape(length, HEADS, FEAT)
    value_f = proj_v.astype(jnp.float32).reshape(length, HEADS, HEAD_DIM)
    own_state, own_norm = block_state(key_f, value_f)
    state_blocks = pack_parts(own_state, own_norm, devices)
    prefix_parts = before_sum(
        lax.all_to_all(state_blocks, "ctx", split_axis=0, concat_axis=0, tiled=True)
    )
    prefix_home = lax.all_to_all(prefix_parts, "ctx", split_axis=0, concat_axis=0, tiled=True)
    prev_state, prev_norm = unpack_parts(prefix_home, own_state, own_norm)
    out_f, back = jax.vjp(block_attend, query_f, key_f, value_f, prev_state, prev_norm)
    mixed = out_f.astype(jnp.bfloat16)
    d_query, d_key, d_value, d_state, d_norm = back(cotangent.astype(jnp.float32))
    d_query = d_query.reshape(length, qk_cols).astype(jnp.bfloat16)
    query_part = lax.dot_general(
        gated, d_query, (((0,), (0,)), ((), ())), preferred_element_type=jnp.float32
    )
    grad_blocks = pack_parts(d_state, d_norm, devices)
    query_part, grad_blocks = lax.optimization_barrier((query_part, grad_blocks))
    grad_query = lax.psum_scatter(query_part, "ctx", scatter_dimension=0, tiled=True)
    suffix_parts = after_sum(
        lax.all_to_all(grad_blocks, "ctx", split_axis=0, concat_axis=0, tiled=True)
    )
    suffix_home = lax.all_to_all(suffix_parts, "ctx", split_axis=0, concat_axis=0, tiled=True)
    later_state, later_norm = unpack_parts(suffix_home, d_state, d_norm)
    later_state, later_norm, grad_query = lax.optimization_barrier((later_state, later_norm, grad_query))
    _, back_state = jax.vjp(block_state, key_f, value_f)
    extra_key, extra_value = back_state((later_state, later_norm))
    d_key = (d_key + extra_key).reshape(length, qk_cols).astype(jnp.bfloat16)
    d_value = (d_value + extra_value).reshape(length, HEADS * HEAD_DIM).astype(jnp.bfloat16)
    d_kv = jnp.concatenate((d_key, d_value), axis=1)
    grads = lax.psum_scatter(
        lax.dot_general(gated, d_kv, (((0,), (0,)), ((), ())), preferred_element_type=jnp.float32),
        "ctx",
        scatter_dimension=0,
        tiled=True,
    )
    contract = (((1,), (1,)), ((), ()))
    d_gated = lax.dot_general(
        jnp.concatenate((d_query, d_key), axis=1), full_qk, contract, preferred_element_type=jnp.float32
    )
    d_gated = d_gated + lax.dot_general(d_value, full_v, contract, preferred_element_type=jnp.float32)
    _, back_conv = jax.vjp(local_gate, tokens_f, rim_f, kernel)
    d_tokens, d_rim, d_kernel = back_conv(d_gated)
    carried = from_behind(d_rim, "ctx", -1)
    d_tokens = jnp.concatenate((d_tokens[: length - 2], d_tokens[length - 2 :] + carried), axis=0)
    kernel_share = lax.psum_scatter(d_kernel, "ctx", scatter_dimension=1, tiled=True)
    return (
        mixed,
        d_tokens.astype(jnp.bfloat16),
        grad_query,
        grads[:, :qk_cols],
        grads[:, qk_cols:],
        kernel_share,
    )


def solution(mesh):
    in_specs = (
        P(("groups", "ctx"), None),
        P(),
        P("ctx", None),
        P("ctx", None),
        P("ctx", None),
        P(("groups", "ctx"), None),
    )
    out_specs = (
        P(("groups", "ctx"), None),
        P(("groups", "ctx"), None),
        P(("groups", "ctx"), None),
        P(("groups", "ctx"), None),
        P(("groups", "ctx"), None),
        P("groups", "ctx"),
    )
    return jax.shard_map(body, mesh=mesh, in_specs=in_specs, out_specs=out_specs, check_vma=False)
```

```python
import jax
import jax.numpy as jnp
import numpy as np
from jax import lax
from jax.sharding import PartitionSpec as P

HEADS = 16
FEAT = 16
HEAD_DIM = 64


def from_behind(value, axis, steps):
    count = lax.axis_size(axis)
    first, last = (max(0, -steps), min(count, count - steps))
    return lax.ppermute(value, axis, [(source, source + steps) for source in range(first, last)])


def pair_tables(feat):
    rows, cols = np.triu_indices(feat)
    coef = np.where(rows == cols, 1.0 / np.sqrt(2.0 * feat), 1.0 / np.sqrt(1.0 * feat))
    return (rows, cols, coef)


def features(block):
    feat = block.shape[-1]
    rows, cols, coef = pair_tables(feat)
    scale = jnp.asarray(coef, jnp.float32)
    eye = np.eye(feat, dtype=np.float32)
    high = lax.Precision.HIGHEST
    pick_rows = jnp.einsum("...f,fp->...p", block, jnp.asarray(eye[:, rows]), precision=high)
    pick_cols = jnp.einsum("...f,fp->...p", block, jnp.asarray(eye[:, cols]), precision=high)
    quad = pick_rows * pick_cols * scale
    ones = jnp.ones(block.shape[:-1] + (1,), jnp.float32)
    return jnp.concatenate((ones, block * feat ** (-0.25), quad), axis=-1)


def block_attend(query, key, value, state, norm):
    length, heads, feat = query.shape
    hdim = value.shape[2]
    width = state.shape[0]
    high = lax.Precision.HIGHEST
    sigma = jnp.einsum("thf,shf->hts", query, key, precision=high) / np.sqrt(1.0 * feat)
    weight = 1.0 + sigma + 0.5 * sigma * sigma
    causal = lax.broadcasted_iota(jnp.int32, (length, length), 0) >= lax.broadcasted_iota(
        jnp.int32, (length, length), 1
    )
    weight = jnp.where(causal[None], weight, jnp.float32(0.0))
    numer = jnp.einsum("hts,she->the", weight, value, precision=high)
    denom = jnp.sum(weight, axis=2).T
    phi_query = features(query)
    numer = numer + jnp.einsum(
        "thn,nhe->the", phi_query, state.reshape(width, heads, hdim), precision=high
    )
    denom = denom + jnp.einsum("thn,nh->th", phi_query, norm, precision=high)
    attended = numer / denom[:, :, None]
    scaled = attended * lax.rsqrt(jnp.mean(attended * attended, axis=2, keepdims=True) + 1e-06)
    return scaled.reshape(length, heads * hdim)


def block_state(key, value):
    length, heads, hdim = value.shape
    phi_key = features(key)
    state = jnp.einsum("shn,she->nhe", phi_key, value, precision=lax.Precision.HIGHEST)
    return (state.reshape(phi_key.shape[2], heads * hdim), jnp.sum(phi_key, axis=0).T)


def pack_parts(state, norm, devices):
    flat = jnp.concatenate((state.reshape(-1), norm.reshape(-1)), axis=0)
    total = flat.shape[0]
    piece = -(-total // (devices * 128)) * 128
    flat = jnp.concatenate((flat, jnp.zeros((devices * piece - total,), jnp.float32)), axis=0)
    return flat.reshape(devices, piece)


def unpack_parts(parts, state, norm):
    flat = parts.reshape(-1)
    count = state.size
    new_state = flat[:count].reshape(state.shape)
    new_norm = flat[count : count + norm.size].reshape(norm.shape)
    return (new_state, new_norm)


def before_sum(block):
    zero_row = jnp.zeros((1, block.shape[1]), jnp.float32)
    return jnp.concatenate((zero_row, jnp.cumsum(block, axis=0)[:-1]), axis=0)


def after_sum(block):
    zero_row = jnp.zeros((1, block.shape[1]), jnp.float32)
    return jnp.concatenate((lax.cumsum(block[1:], axis=0, reverse=True), zero_row), axis=0)


def local_gate(tokens_f, rim_f, kernel):
    padded = jnp.concatenate((rim_f, tokens_f), axis=0)
    conv = kernel[0] * padded[2:] + kernel[1] * padded[1:-1] + kernel[2] * padded[:-2]
    return tokens_f + jax.nn.sigmoid(tokens_f) * conv


def body(tokens, kernel, w_query, w_key, w_value, cotangent):
    length = tokens.shape[0]
    qk_cols = w_query.shape[1]
    devices = lax.axis_size("ctx")
    rim = from_behind(tokens[length - 2 :], "ctx", 1)
    tokens_f = tokens.astype(jnp.float32)
    rim_f = rim.astype(jnp.float32)
    gated = local_gate(tokens_f, rim_f, kernel).astype(jnp.bfloat16)
    stacked = lax.all_gather(
        jnp.concatenate((w_query, w_key, w_value), axis=1), "ctx", axis=0, tiled=True
    )
    full_qk = stacked[:, : 2 * qk_cols]
    full_v = stacked[:, 2 * qk_cols :]
    proj_qk = jnp.dot(gated, full_qk, preferred_element_type=jnp.float32).astype(jnp.bfloat16)
    proj_v = jnp.dot(gated, full_v, preferred_element_type=jnp.float32).astype(jnp.bfloat16)
    query_f = proj_qk[:, :qk_cols].astype(jnp.float32).reshape(length, HEADS, FEAT)
    key_f = proj_qk[:, qk_cols:].astype(jnp.float32).reshape(length, HEADS, FEAT)
    value_f = proj_v.astype(jnp.float32).reshape(length, HEADS, HEAD_DIM)
    own_state, own_norm = block_state(key_f, value_f)
    state_blocks = pack_parts(own_state, own_norm, devices)
    prefix_parts = before_sum(
        lax.all_to_all(state_blocks, "ctx", split_axis=0, concat_axis=0, tiled=True)
    )
    prefix_home = lax.all_to_all(prefix_parts, "ctx", split_axis=0, concat_axis=0, tiled=True)
    prev_state, prev_norm = unpack_parts(prefix_home, own_state, own_norm)
    out_f, back = jax.vjp(block_attend, query_f, key_f, value_f, prev_state, prev_norm)
    mixed = out_f.astype(jnp.bfloat16)
    d_query, d_key, d_value, d_state, d_norm = back(cotangent.astype(jnp.float32))
    d_query = d_query.reshape(length, qk_cols).astype(jnp.bfloat16)
    query_part = lax.dot_general(
        gated, d_query, (((0,), (0,)), ((), ())), preferred_element_type=jnp.float32
    )
    grad_blocks = pack_parts(d_state, d_norm, devices)
    query_part, grad_blocks = lax.optimization_barrier((query_part, grad_blocks))
    grad_query = lax.psum_scatter(query_part, "ctx", scatter_dimension=0, tiled=True)
    suffix_parts = after_sum(
        lax.all_to_all(grad_blocks, "ctx", split_axis=0, concat_axis=0, tiled=True)
    )
    suffix_home = lax.all_to_all(suffix_parts, "ctx", split_axis=0, concat_axis=0, tiled=True)
    later_state, later_norm = unpack_parts(suffix_home, d_state, d_norm)
    later_state, later_norm, grad_query = lax.optimization_barrier((later_state, later_norm, grad_query))
    _, back_state = jax.vjp(block_state, key_f, value_f)
    extra_key, extra_value = back_state((later_state, later_norm))
    d_key = (d_key + extra_key).reshape(length, qk_cols).astype(jnp.bfloat16)
    d_value = (d_value + extra_value).reshape(length, HEADS * HEAD_DIM).astype(jnp.bfloat16)
    d_kv = jnp.concatenate((d_key, d_value), axis=1)
    grads = lax.psum_scatter(
        lax.dot_general(gated, d_kv, (((0,), (0,)), ((), ())), preferred_element_type=jnp.float32),
        "ctx",
        scatter_dimension=0,
        tiled=True,
    )
    contract = (((1,), (1,)), ((), ()))
    d_gated = lax.dot_general(
        jnp.concatenate((d_query, d_key), axis=1), full_qk, contract, preferred_element_type=jnp.float32
    )
    d_gated = d_gated + lax.dot_general(d_value, full_v, contract, preferred_element_type=jnp.float32)
    _, back_conv = jax.vjp(local_gate, tokens_f, rim_f, kernel)
    d_tokens, d_rim, d_kernel = back_conv(d_gated)
    carried = from_behind(d_rim, "ctx", -1)
    d_tokens = jnp.concatenate((d_tokens[: length - 2], d_tokens[length - 2 :] + carried), axis=0)
    taps, width = d_kernel.shape
    d_kernel = d_kernel.reshape(taps, devices, width // devices).transpose(1, 0, 2)
    kernel_share = lax.psum_scatter(
        d_kernel.reshape(devices * taps, width // devices), "ctx", scatter_dimension=0, tiled=True
    )
    return (
        mixed,
        d_tokens.astype(jnp.bfloat16),
        grad_query,
        grads[:, :qk_cols],
        grads[:, qk_cols:],
        kernel_share,
    )


def solution(mesh):
    in_specs = (
        P(("groups", "ctx"), None),
        P(),
        P("ctx", None),
        P("ctx", None),
        P("ctx", None),
        P(("groups", "ctx"), None),
    )
    out_specs = (
        P(("groups", "ctx"), None),
        P(("groups", "ctx"), None),
        P(("groups", "ctx"), None),
        P(("groups", "ctx"), None),
        P(("groups", "ctx"), None),
        P("groups", "ctx"),
    )
    return jax.shard_map(body, mesh=mesh, in_specs=in_specs, out_specs=out_specs, check_vma=False)
```

```python
import jax
import jax.numpy as jnp
import numpy as np
from jax import lax
from jax.sharding import PartitionSpec as P

HEADS = 16
FEAT = 16
HEAD_DIM = 64


def from_behind(value, axis, steps):
    count = lax.axis_size(axis)
    first, last = (max(0, -steps), min(count, count - steps))
    return lax.ppermute(value, axis, [(source, source + steps) for source in range(first, last)])


def pair_tables(feat):
    rows, cols = np.triu_indices(feat)
    coef = np.where(rows == cols, 1.0 / np.sqrt(2.0 * feat), 1.0 / np.sqrt(1.0 * feat))
    return (rows, cols, coef)


def features(block):
    feat = block.shape[-1]
    rows, cols, coef = pair_tables(feat)
    scale = jnp.asarray(coef, jnp.float32)
    eye = np.eye(feat, dtype=np.float32)
    high = lax.Precision.HIGHEST
    pick_rows = jnp.einsum("...f,fp->...p", block, jnp.asarray(eye[:, rows]), precision=high)
    pick_cols = jnp.einsum("...f,fp->...p", block, jnp.asarray(eye[:, cols]), precision=high)
    quad = pick_rows * pick_cols * scale
    ones = jnp.ones(block.shape[:-1] + (1,), jnp.float32)
    return jnp.concatenate((ones, block * feat ** (-0.25), quad), axis=-1)


def block_attend(query, key, value, state, norm):
    length, heads, feat = query.shape
    hdim = value.shape[2]
    width = state.shape[0]
    high = lax.Precision.HIGHEST
    sigma = jnp.einsum("thf,shf->hts", query, key, precision=high) / np.sqrt(1.0 * feat)
    weight = 1.0 + sigma + 0.5 * sigma * sigma
    causal = lax.broadcasted_iota(jnp.int32, (length, length), 0) >= lax.broadcasted_iota(
        jnp.int32, (length, length), 1
    )
    weight = jnp.where(causal[None], weight, jnp.float32(0.0))
    numer = jnp.einsum("hts,she->the", weight, value, precision=high)
    denom = jnp.sum(weight, axis=2).T
    phi_query = features(query)
    numer = numer + jnp.einsum(
        "thn,nhe->the", phi_query, state.reshape(width, heads, hdim), precision=high
    )
    denom = denom + jnp.einsum("thn,nh->th", phi_query, norm, precision=high)
    attended = numer / denom[:, :, None]
    scaled = attended * lax.rsqrt(jnp.mean(attended * attended, axis=2, keepdims=True) + 1e-06)
    return scaled.reshape(length, heads * hdim)


def block_state(key, value):
    length, heads, hdim = value.shape
    phi_key = features(key)
    state = jnp.einsum("shn,she->nhe", phi_key, value, precision=lax.Precision.HIGHEST)
    return (state.reshape(phi_key.shape[2], heads * hdim), jnp.sum(phi_key, axis=0).T)


def pack_parts(state, norm, devices):
    flat = jnp.concatenate((state.reshape(-1), norm.reshape(-1)), axis=0)
    total = flat.shape[0]
    piece = -(-total // (devices * 128)) * 128
    flat = jnp.concatenate((flat, jnp.zeros((devices * piece - total,), jnp.float32)), axis=0)
    return flat.reshape(devices, piece)


def unpack_parts(parts, state, norm):
    flat = parts.reshape(-1)
    count = state.size
    new_state = flat[:count].reshape(state.shape)
    new_norm = flat[count : count + norm.size].reshape(norm.shape)
    return (new_state, new_norm)


def before_sum(block):
    zero_row = jnp.zeros((1, block.shape[1]), jnp.float32)
    return jnp.concatenate((zero_row, jnp.cumsum(block, axis=0)[:-1]), axis=0)


def after_sum(block):
    zero_row = jnp.zeros((1, block.shape[1]), jnp.float32)
    return jnp.concatenate((lax.cumsum(block[1:], axis=0, reverse=True), zero_row), axis=0)


def exclusive_scan(parts, axis, direction):
    count = lax.axis_size(axis)
    total = parts
    step = 1
    while step < count:
        if direction > 0:
            pairs = [(source, source + step) for source in range(count - step)]
        else:
            pairs = [(source + step, source) for source in range(count - step)]
        moved = lax.ppermute(total, axis, pairs)
        total = jax.tree.map(jnp.add, total, moved)
        step *= 2
    return jax.tree.map(jnp.subtract, total, parts)


def local_gate(tokens_f, rim_f, kernel):
    padded = jnp.concatenate((rim_f, tokens_f), axis=0)
    conv = kernel[0] * padded[2:] + kernel[1] * padded[1:-1] + kernel[2] * padded[:-2]
    return tokens_f + jax.nn.sigmoid(tokens_f) * conv


def body(tokens, kernel, w_query, w_key, w_value, cotangent):
    length = tokens.shape[0]
    qk_cols = w_query.shape[1]
    devices = lax.axis_size("ctx")
    rim = from_behind(tokens[length - 2 :], "ctx", 1)
    tokens_f = tokens.astype(jnp.float32)
    rim_f = rim.astype(jnp.float32)
    gated = local_gate(tokens_f, rim_f, kernel).astype(jnp.bfloat16)
    stacked = lax.all_gather(
        jnp.concatenate((w_query, w_key, w_value), axis=1), "ctx", axis=0, tiled=True
    )
    full_qk = stacked[:, : 2 * qk_cols]
    full_v = stacked[:, 2 * qk_cols :]
    proj_qk = jnp.dot(gated, full_qk, preferred_element_type=jnp.float32).astype(jnp.bfloat16)
    proj_v = jnp.dot(gated, full_v, preferred_element_type=jnp.float32).astype(jnp.bfloat16)
    query_f = proj_qk[:, :qk_cols].astype(jnp.float32).reshape(length, HEADS, FEAT)
    key_f = proj_qk[:, qk_cols:].astype(jnp.float32).reshape(length, HEADS, FEAT)
    value_f = proj_v.astype(jnp.float32).reshape(length, HEADS, HEAD_DIM)
    own_state, own_norm = block_state(key_f, value_f)
    prev_state, prev_norm = exclusive_scan((own_state, own_norm), "ctx", 1)
    out_f, back = jax.vjp(block_attend, query_f, key_f, value_f, prev_state, prev_norm)
    mixed = out_f.astype(jnp.bfloat16)
    d_query, d_key, d_value, d_state, d_norm = back(cotangent.astype(jnp.float32))
    d_query = d_query.reshape(length, qk_cols).astype(jnp.bfloat16)
    query_part = lax.dot_general(
        gated, d_query, (((0,), (0,)), ((), ())), preferred_element_type=jnp.float32
    )
    query_part, d_state, d_norm = lax.optimization_barrier((query_part, d_state, d_norm))
    grad_query = lax.psum_scatter(query_part, "ctx", scatter_dimension=0, tiled=True)
    later_state, later_norm = exclusive_scan((d_state, d_norm), "ctx", -1)
    later_state, later_norm, grad_query = lax.optimization_barrier((later_state, later_norm, grad_query))
    _, back_state = jax.vjp(block_state, key_f, value_f)
    extra_key, extra_value = back_state((later_state, later_norm))
    d_key = (d_key + extra_key).reshape(length, qk_cols).astype(jnp.bfloat16)
    d_value = (d_value + extra_value).reshape(length, HEADS * HEAD_DIM).astype(jnp.bfloat16)
    d_kv = jnp.concatenate((d_key, d_value), axis=1)
    grads = lax.psum_scatter(
        lax.dot_general(gated, d_kv, (((0,), (0,)), ((), ())), preferred_element_type=jnp.float32),
        "ctx",
        scatter_dimension=0,
        tiled=True,
    )
    contract = (((1,), (1,)), ((), ()))
    d_gated = lax.dot_general(
        jnp.concatenate((d_query, d_key), axis=1), full_qk, contract, preferred_element_type=jnp.float32
    )
    d_gated = d_gated + lax.dot_general(d_value, full_v, contract, preferred_element_type=jnp.float32)
    _, back_conv = jax.vjp(local_gate, tokens_f, rim_f, kernel)
    d_tokens, d_rim, d_kernel = back_conv(d_gated)
    carried = from_behind(d_rim, "ctx", -1)
    d_tokens = jnp.concatenate((d_tokens[: length - 2], d_tokens[length - 2 :] + carried), axis=0)
    taps, width = d_kernel.shape
    d_kernel = d_kernel.reshape(taps, devices, width // devices).transpose(1, 0, 2)
    kernel_share = lax.psum_scatter(
        d_kernel.reshape(devices * taps, width // devices), "ctx", scatter_dimension=0, tiled=True
    )
    return (
        mixed,
        d_tokens.astype(jnp.bfloat16),
        grad_query,
        grads[:, :qk_cols],
        grads[:, qk_cols:],
        kernel_share,
    )


def solution(mesh):
    in_specs = (
        P(("groups", "ctx"), None),
        P(),
        P("ctx", None),
        P("ctx", None),
        P("ctx", None),
        P(("groups", "ctx"), None),
    )
    out_specs = (
        P(("groups", "ctx"), None),
        P(("groups", "ctx"), None),
        P(("groups", "ctx"), None),
        P(("groups", "ctx"), None),
        P(("groups", "ctx"), None),
        P("groups", "ctx"),
    )
    return jax.shard_map(body, mesh=mesh, in_specs=in_specs, out_specs=out_specs, check_vma=False)
```

```python
import jax
import jax.numpy as jnp
import numpy as np
from jax import lax
from jax.sharding import PartitionSpec as P

HEADS = 16
FEAT = 16
HEAD_DIM = 64


def from_behind(value, axis, steps):
    count = lax.axis_size(axis)
    first, last = (max(0, -steps), min(count, count - steps))
    return lax.ppermute(value, axis, [(source, source + steps) for source in range(first, last)])


def pair_tables(feat):
    rows, cols = np.triu_indices(feat)
    coef = np.where(rows == cols, 1.0 / np.sqrt(2.0 * feat), 1.0 / np.sqrt(1.0 * feat))
    return (rows, cols, coef)


def features(block):
    feat = block.shape[-1]
    rows, cols, coef = pair_tables(feat)
    scale = jnp.asarray(coef, jnp.float32)
    eye = np.eye(feat, dtype=np.float32)
    high = lax.Precision.HIGHEST
    pick_rows = jnp.einsum("...f,fp->...p", block, jnp.asarray(eye[:, rows]), precision=high)
    pick_cols = jnp.einsum("...f,fp->...p", block, jnp.asarray(eye[:, cols]), precision=high)
    quad = pick_rows * pick_cols * scale
    ones = jnp.ones(block.shape[:-1] + (1,), jnp.float32)
    return jnp.concatenate((ones, block * feat ** (-0.25), quad), axis=-1)


def block_attend(query, key, value, state, norm):
    length, heads, feat = query.shape
    hdim = value.shape[2]
    width = state.shape[0]
    high = lax.Precision.HIGHEST
    sigma = jnp.einsum("thf,shf->hts", query, key, precision=high) / np.sqrt(1.0 * feat)
    weight = 1.0 + sigma + 0.5 * sigma * sigma
    causal = lax.broadcasted_iota(jnp.int32, (length, length), 0) >= lax.broadcasted_iota(
        jnp.int32, (length, length), 1
    )
    weight = jnp.where(causal[None], weight, jnp.float32(0.0))
    numer = jnp.einsum("hts,she->the", weight, value, precision=high)
    denom = jnp.sum(weight, axis=2).T
    phi_query = features(query)
    numer = numer + jnp.einsum(
        "thn,nhe->the", phi_query, state.reshape(width, heads, hdim), precision=high
    )
    denom = denom + jnp.einsum("thn,nh->th", phi_query, norm, precision=high)
    attended = numer / denom[:, :, None]
    scaled = attended * lax.rsqrt(jnp.mean(attended * attended, axis=2, keepdims=True) + 1e-06)
    return scaled.reshape(length, heads * hdim)


def block_state(key, value):
    length, heads, hdim = value.shape
    phi_key = features(key)
    state = jnp.einsum("shn,she->nhe", phi_key, value, precision=lax.Precision.HIGHEST)
    return (state.reshape(phi_key.shape[2], heads * hdim), jnp.sum(phi_key, axis=0).T)


def pack_parts(state, norm, devices):
    flat = jnp.concatenate((state.reshape(-1), norm.reshape(-1)), axis=0)
    total = flat.shape[0]
    piece = -(-total // (devices * 128)) * 128
    flat = jnp.concatenate((flat, jnp.zeros((devices * piece - total,), jnp.float32)), axis=0)
    return flat.reshape(devices, piece)


def unpack_parts(parts, state, norm):
    flat = parts.reshape(-1)
    count = state.size
    new_state = flat[:count].reshape(state.shape)
    new_norm = flat[count : count + norm.size].reshape(norm.shape)
    return (new_state, new_norm)


def before_sum(block):
    zero_row = jnp.zeros((1, block.shape[1]), jnp.float32)
    return jnp.concatenate((zero_row, jnp.cumsum(block, axis=0)[:-1]), axis=0)


def after_sum(block):
    zero_row = jnp.zeros((1, block.shape[1]), jnp.float32)
    return jnp.concatenate((lax.cumsum(block[1:], axis=0, reverse=True), zero_row), axis=0)


def exclusive_scan(parts, axis, direction):
    count = lax.axis_size(axis)
    state, norm = parts
    joined = jnp.concatenate((state, norm), axis=1)
    total = joined
    step = 1
    while step < count:
        if direction > 0:
            pairs = [(source, source + step) for source in range(count - step)]
        else:
            pairs = [(source + step, source) for source in range(count - step)]
        total = total + lax.ppermute(total, axis, pairs)
        step *= 2
    total = total - joined
    return (total[:, : state.shape[1]], total[:, state.shape[1] :])


def local_gate(tokens_f, rim_f, kernel):
    padded = jnp.concatenate((rim_f, tokens_f), axis=0)
    conv = kernel[0] * padded[2:] + kernel[1] * padded[1:-1] + kernel[2] * padded[:-2]
    return tokens_f + jax.nn.sigmoid(tokens_f) * conv


def body(tokens, kernel, w_query, w_key, w_value, cotangent):
    length = tokens.shape[0]
    qk_cols = w_query.shape[1]
    devices = lax.axis_size("ctx")
    rim = from_behind(tokens[length - 2 :], "ctx", 1)
    tokens_f = tokens.astype(jnp.float32)
    rim_f = rim.astype(jnp.float32)
    gated = local_gate(tokens_f, rim_f, kernel).astype(jnp.bfloat16)
    stacked = lax.all_gather(
        jnp.concatenate((w_query, w_key, w_value), axis=1), "ctx", axis=0, tiled=True
    )
    full_qk = stacked[:, : 2 * qk_cols]
    full_v = stacked[:, 2 * qk_cols :]
    proj_qk = jnp.dot(gated, full_qk, preferred_element_type=jnp.float32).astype(jnp.bfloat16)
    proj_v = jnp.dot(gated, full_v, preferred_element_type=jnp.float32).astype(jnp.bfloat16)
    query_f = proj_qk[:, :qk_cols].astype(jnp.float32).reshape(length, HEADS, FEAT)
    key_f = proj_qk[:, qk_cols:].astype(jnp.float32).reshape(length, HEADS, FEAT)
    value_f = proj_v.astype(jnp.float32).reshape(length, HEADS, HEAD_DIM)
    own_state, own_norm = block_state(key_f, value_f)
    prev_state, prev_norm = exclusive_scan((own_state, own_norm), "ctx", 1)
    out_f, back = jax.vjp(block_attend, query_f, key_f, value_f, prev_state, prev_norm)
    mixed = out_f.astype(jnp.bfloat16)
    d_query, d_key, d_value, d_state, d_norm = back(cotangent.astype(jnp.float32))
    d_query = d_query.reshape(length, qk_cols).astype(jnp.bfloat16)
    query_part = lax.dot_general(
        gated, d_query, (((0,), (0,)), ((), ())), preferred_element_type=jnp.float32
    )
    query_part, d_state, d_norm = lax.optimization_barrier((query_part, d_state, d_norm))
    grad_query = lax.psum_scatter(query_part, "ctx", scatter_dimension=0, tiled=True)
    later_state, later_norm = exclusive_scan((d_state, d_norm), "ctx", -1)
    later_state, later_norm, grad_query = lax.optimization_barrier((later_state, later_norm, grad_query))
    _, back_state = jax.vjp(block_state, key_f, value_f)
    extra_key, extra_value = back_state((later_state, later_norm))
    d_key = (d_key + extra_key).reshape(length, qk_cols).astype(jnp.bfloat16)
    d_value = (d_value + extra_value).reshape(length, HEADS * HEAD_DIM).astype(jnp.bfloat16)
    d_kv = jnp.concatenate((d_key, d_value), axis=1)
    grads = lax.psum_scatter(
        lax.dot_general(gated, d_kv, (((0,), (0,)), ((), ())), preferred_element_type=jnp.float32),
        "ctx",
        scatter_dimension=0,
        tiled=True,
    )
    contract = (((1,), (1,)), ((), ()))
    d_gated = lax.dot_general(
        jnp.concatenate((d_query, d_key), axis=1), full_qk, contract, preferred_element_type=jnp.float32
    )
    d_gated = d_gated + lax.dot_general(d_value, full_v, contract, preferred_element_type=jnp.float32)
    _, back_conv = jax.vjp(local_gate, tokens_f, rim_f, kernel)
    d_tokens, d_rim, d_kernel = back_conv(d_gated)
    carried = from_behind(d_rim, "ctx", -1)
    d_tokens = jnp.concatenate((d_tokens[: length - 2], d_tokens[length - 2 :] + carried), axis=0)
    taps, width = d_kernel.shape
    d_kernel = d_kernel.reshape(taps, devices, width // devices).transpose(1, 0, 2)
    kernel_share = lax.psum_scatter(
        d_kernel.reshape(devices * taps, width // devices), "ctx", scatter_dimension=0, tiled=True
    )
    return (
        mixed,
        d_tokens.astype(jnp.bfloat16),
        grad_query,
        grads[:, :qk_cols],
        grads[:, qk_cols:],
        kernel_share,
    )


def solution(mesh):
    in_specs = (
        P(("groups", "ctx"), None),
        P(),
        P("ctx", None),
        P("ctx", None),
        P("ctx", None),
        P(("groups", "ctx"), None),
    )
    out_specs = (
        P(("groups", "ctx"), None),
        P(("groups", "ctx"), None),
        P(("groups", "ctx"), None),
        P(("groups", "ctx"), None),
        P(("groups", "ctx"), None),
        P("groups", "ctx"),
    )
    return jax.shard_map(body, mesh=mesh, in_specs=in_specs, out_specs=out_specs, check_vma=False)
```

```python
import jax
import jax.numpy as jnp
import numpy as np
from jax import lax
from jax.sharding import PartitionSpec as P

HEADS = 16
FEAT = 16
HEAD_DIM = 64


def from_behind(value, axis, steps):
    count = lax.axis_size(axis)
    first, last = (max(0, -steps), min(count, count - steps))
    return lax.ppermute(value, axis, [(source, source + steps) for source in range(first, last)])


def pair_tables(feat):
    rows, cols = np.triu_indices(feat)
    coef = np.where(rows == cols, 1.0 / np.sqrt(2.0 * feat), 1.0 / np.sqrt(1.0 * feat))
    return (rows, cols, coef)


def features(block):
    feat = block.shape[-1]
    rows, cols, coef = pair_tables(feat)
    scale = jnp.asarray(coef, jnp.float32)
    eye = np.eye(feat, dtype=np.float32)
    high = lax.Precision.HIGHEST
    pick_rows = jnp.einsum("...f,fp->...p", block, jnp.asarray(eye[:, rows]), precision=high)
    pick_cols = jnp.einsum("...f,fp->...p", block, jnp.asarray(eye[:, cols]), precision=high)
    quad = pick_rows * pick_cols * scale
    ones = jnp.ones(block.shape[:-1] + (1,), jnp.float32)
    return jnp.concatenate((ones, block * feat ** (-0.25), quad), axis=-1)


def block_attend(query, key, value, state, norm):
    length, heads, feat = query.shape
    hdim = value.shape[2]
    width = state.shape[0]
    high = lax.Precision.HIGHEST
    sigma = jnp.einsum("thf,shf->hts", query, key, precision=high) / np.sqrt(1.0 * feat)
    weight = 1.0 + sigma + 0.5 * sigma * sigma
    causal = lax.broadcasted_iota(jnp.int32, (length, length), 0) >= lax.broadcasted_iota(
        jnp.int32, (length, length), 1
    )
    weight = jnp.where(causal[None], weight, jnp.float32(0.0))
    numer = jnp.einsum("hts,she->the", weight, value, precision=high)
    denom = jnp.sum(weight, axis=2).T
    phi_query = features(query)
    numer = numer + jnp.einsum(
        "thn,nhe->the", phi_query, state.reshape(width, heads, hdim), precision=high
    )
    denom = denom + jnp.einsum("thn,nh->th", phi_query, norm, precision=high)
    attended = numer / denom[:, :, None]
    scaled = attended * lax.rsqrt(jnp.mean(attended * attended, axis=2, keepdims=True) + 1e-06)
    return scaled.reshape(length, heads * hdim)


def block_state(key, value):
    length, heads, hdim = value.shape
    phi_key = features(key)
    state = jnp.einsum("shn,she->nhe", phi_key, value, precision=lax.Precision.HIGHEST)
    return (state.reshape(phi_key.shape[2], heads * hdim), jnp.sum(phi_key, axis=0).T)


def pack_parts(state, norm, devices):
    flat = jnp.concatenate((state.reshape(-1), norm.reshape(-1)), axis=0)
    total = flat.shape[0]
    piece = -(-total // (devices * 128)) * 128
    flat = jnp.concatenate((flat, jnp.zeros((devices * piece - total,), jnp.float32)), axis=0)
    return flat.reshape(devices, piece)


def unpack_parts(parts, state, norm):
    flat = parts.reshape(-1)
    count = state.size
    new_state = flat[:count].reshape(state.shape)
    new_norm = flat[count : count + norm.size].reshape(norm.shape)
    return (new_state, new_norm)


def before_sum(block):
    zero_row = jnp.zeros((1, block.shape[1]), jnp.float32)
    return jnp.concatenate((zero_row, jnp.cumsum(block, axis=0)[:-1]), axis=0)


def after_sum(block):
    zero_row = jnp.zeros((1, block.shape[1]), jnp.float32)
    return jnp.concatenate((lax.cumsum(block[1:], axis=0, reverse=True), zero_row), axis=0)


def exclusive_scan(parts, axis, direction):
    count = lax.axis_size(axis)
    state, norm = parts
    joined = jnp.concatenate((state, norm), axis=1)
    total = joined
    step = 1
    while step < count:
        if direction > 0:
            pairs = [(source, source + step) for source in range(count - step)]
        else:
            pairs = [(source + step, source) for source in range(count - step)]
        total = total + lax.ppermute(total, axis, pairs)
        step *= 2
    total = total - joined
    return (total[:, : state.shape[1]], total[:, state.shape[1] :])


def local_gate(tokens_f, rim_f, kernel):
    padded = jnp.concatenate((rim_f, tokens_f), axis=0)
    conv = kernel[0] * padded[2:] + kernel[1] * padded[1:-1] + kernel[2] * padded[:-2]
    return tokens_f + jax.nn.sigmoid(tokens_f) * conv


def body(tokens, kernel, w_query, w_key, w_value, cotangent):
    length = tokens.shape[0]
    qk_cols = w_query.shape[1]
    devices = lax.axis_size("ctx")
    rim = from_behind(tokens[length - 2 :], "ctx", 1)
    tokens_f = tokens.astype(jnp.float32)
    rim_f = rim.astype(jnp.float32)
    gated = local_gate(tokens_f, rim_f, kernel).astype(jnp.bfloat16)
    stacked = lax.all_gather(
        jnp.concatenate((w_query, w_key, w_value), axis=1), "ctx", axis=0, tiled=True
    )
    full_qk = stacked[:, : 2 * qk_cols]
    full_v = stacked[:, 2 * qk_cols :]
    proj_qk = jnp.dot(gated, full_qk, preferred_element_type=jnp.float32).astype(jnp.bfloat16)
    proj_v = jnp.dot(gated, full_v, preferred_element_type=jnp.float32).astype(jnp.bfloat16)
    query_f = proj_qk[:, :qk_cols].astype(jnp.float32).reshape(length, HEADS, FEAT)
    key_f = proj_qk[:, qk_cols:].astype(jnp.float32).reshape(length, HEADS, FEAT)
    value_f = proj_v.astype(jnp.float32).reshape(length, HEADS, HEAD_DIM)
    own_state, own_norm = block_state(key_f, value_f)
    prev_state, prev_norm = exclusive_scan((own_state, own_norm), "ctx", 1)
    out_f, back = jax.vjp(block_attend, query_f, key_f, value_f, prev_state, prev_norm)
    mixed = out_f.astype(jnp.bfloat16)
    d_query, d_key, d_value, d_state, d_norm = back(cotangent.astype(jnp.float32))
    d_query = d_query.reshape(length, qk_cols).astype(jnp.bfloat16)
    query_part = lax.dot_general(
        gated, d_query, (((0,), (0,)), ((), ())), preferred_element_type=jnp.float32
    )
    later_state, later_norm = exclusive_scan((d_state, d_norm), "ctx", -1)
    query_part, later_state, later_norm = lax.optimization_barrier((query_part, later_state, later_norm))
    grad_query = lax.psum_scatter(query_part, "ctx", scatter_dimension=0, tiled=True)
    _, back_state = jax.vjp(block_state, key_f, value_f)
    extra_key, extra_value = back_state((later_state, later_norm))
    d_key = (d_key + extra_key).reshape(length, qk_cols).astype(jnp.bfloat16)
    d_value = (d_value + extra_value).reshape(length, HEADS * HEAD_DIM).astype(jnp.bfloat16)
    d_kv = jnp.concatenate((d_key, d_value), axis=1)
    grads = lax.psum_scatter(
        lax.dot_general(gated, d_kv, (((0,), (0,)), ((), ())), preferred_element_type=jnp.float32),
        "ctx",
        scatter_dimension=0,
        tiled=True,
    )
    contract = (((1,), (1,)), ((), ()))
    d_gated = lax.dot_general(
        jnp.concatenate((d_query, d_key), axis=1), full_qk, contract, preferred_element_type=jnp.float32
    )
    d_gated = d_gated + lax.dot_general(d_value, full_v, contract, preferred_element_type=jnp.float32)
    _, back_conv = jax.vjp(local_gate, tokens_f, rim_f, kernel)
    d_tokens, d_rim, d_kernel = back_conv(d_gated)
    carried = from_behind(d_rim, "ctx", -1)
    d_tokens = jnp.concatenate((d_tokens[: length - 2], d_tokens[length - 2 :] + carried), axis=0)
    taps, width = d_kernel.shape
    d_kernel = d_kernel.reshape(taps, devices, width // devices).transpose(1, 0, 2)
    kernel_share = lax.psum_scatter(
        d_kernel.reshape(devices * taps, width // devices), "ctx", scatter_dimension=0, tiled=True
    )
    return (
        mixed,
        d_tokens.astype(jnp.bfloat16),
        grad_query,
        grads[:, :qk_cols],
        grads[:, qk_cols:],
        kernel_share,
    )


def solution(mesh):
    in_specs = (
        P(("groups", "ctx"), None),
        P(),
        P("ctx", None),
        P("ctx", None),
        P("ctx", None),
        P(("groups", "ctx"), None),
    )
    out_specs = (
        P(("groups", "ctx"), None),
        P(("groups", "ctx"), None),
        P(("groups", "ctx"), None),
        P(("groups", "ctx"), None),
        P(("groups", "ctx"), None),
        P("groups", "ctx"),
    )
    return jax.shard_map(body, mesh=mesh, in_specs=in_specs, out_specs=out_specs, check_vma=False)
```

```python
import jax
import jax.numpy as jnp
import numpy as np
from jax import lax
from jax.sharding import PartitionSpec as P

HEADS = 16
FEAT = 16
HEAD_DIM = 64


def from_behind(value, axis, steps):
    count = lax.axis_size(axis)
    first, last = (max(0, -steps), min(count, count - steps))
    return lax.ppermute(value, axis, [(source, source + steps) for source in range(first, last)])


def pair_tables(feat):
    rows, cols = np.triu_indices(feat)
    coef = np.where(rows == cols, 1.0 / np.sqrt(2.0 * feat), 1.0 / np.sqrt(1.0 * feat))
    return (rows, cols, coef)


def features(block):
    feat = block.shape[-1]
    rows, cols, coef = pair_tables(feat)
    scale = jnp.asarray(coef, jnp.float32)
    eye = np.eye(feat, dtype=np.float32)
    high = lax.Precision.HIGHEST
    pick_rows = jnp.einsum("...f,fp->...p", block, jnp.asarray(eye[:, rows]), precision=high)
    pick_cols = jnp.einsum("...f,fp->...p", block, jnp.asarray(eye[:, cols]), precision=high)
    quad = pick_rows * pick_cols * scale
    ones = jnp.ones(block.shape[:-1] + (1,), jnp.float32)
    return jnp.concatenate((ones, block * feat ** (-0.25), quad), axis=-1)


def block_attend(query, key, value, state, norm):
    length, heads, feat = query.shape
    hdim = value.shape[2]
    width = state.shape[0]
    high = lax.Precision.HIGHEST
    sigma = jnp.einsum("thf,shf->hts", query, key, precision=high) / np.sqrt(1.0 * feat)
    weight = 1.0 + sigma + 0.5 * sigma * sigma
    causal = lax.broadcasted_iota(jnp.int32, (length, length), 0) >= lax.broadcasted_iota(
        jnp.int32, (length, length), 1
    )
    weight = jnp.where(causal[None], weight, jnp.float32(0.0))
    numer = jnp.einsum("hts,she->the", weight, value, precision=high)
    denom = jnp.sum(weight, axis=2).T
    phi_query = features(query)
    numer = numer + jnp.einsum(
        "thn,nhe->the", phi_query, state.reshape(width, heads, hdim), precision=high
    )
    denom = denom + jnp.einsum("thn,nh->th", phi_query, norm, precision=high)
    attended = numer / denom[:, :, None]
    scaled = attended * lax.rsqrt(jnp.mean(attended * attended, axis=2, keepdims=True) + 1e-06)
    return scaled.reshape(length, heads * hdim)


def block_state(key, value):
    length, heads, hdim = value.shape
    phi_key = features(key)
    state = jnp.einsum("shn,she->nhe", phi_key, value, precision=lax.Precision.HIGHEST)
    return (state.reshape(phi_key.shape[2], heads * hdim), jnp.sum(phi_key, axis=0).T)


def pack_parts(state, norm, devices):
    feat, cols = state.shape
    rows = -(-feat // 40) * 40
    spare = (rows - feat) * cols
    flat = norm.reshape(-1)
    flat = jnp.concatenate((flat, jnp.zeros((spare - flat.shape[0],), jnp.float32)), axis=0)
    block = jnp.concatenate((state, flat.reshape(rows - feat, cols)), axis=0)
    row_parts = rows // 40
    col_parts = devices // row_parts
    block = block.reshape(row_parts, 40, col_parts, cols // col_parts).transpose(0, 2, 1, 3)
    return block.reshape(devices, 40, cols // col_parts)


def unpack_parts(parts, state, norm):
    feat, cols = state.shape
    devices, tall, wide = parts.shape
    col_parts = cols // wide
    row_parts = devices // col_parts
    block = parts.reshape(row_parts, col_parts, tall, wide).transpose(0, 2, 1, 3)
    block = block.reshape(row_parts * tall, cols)
    new_state = block[:feat]
    new_norm = block[feat:].reshape(-1)[: norm.size].reshape(norm.shape)
    return (new_state, new_norm)


def before_sum(block):
    zero_row = jnp.zeros((1,) + block.shape[1:], jnp.float32)
    return jnp.concatenate((zero_row, jnp.cumsum(block, axis=0)[:-1]), axis=0)


def after_sum(block):
    zero_row = jnp.zeros((1,) + block.shape[1:], jnp.float32)
    return jnp.concatenate((lax.cumsum(block[1:], axis=0, reverse=True), zero_row), axis=0)


def local_gate(tokens_f, rim_f, kernel):
    padded = jnp.concatenate((rim_f, tokens_f), axis=0)
    conv = kernel[0] * padded[2:] + kernel[1] * padded[1:-1] + kernel[2] * padded[:-2]
    return tokens_f + jax.nn.sigmoid(tokens_f) * conv


def body(tokens, kernel, w_query, w_key, w_value, cotangent):
    length = tokens.shape[0]
    qk_cols = w_query.shape[1]
    devices = lax.axis_size("ctx")
    rim = from_behind(tokens[length - 2 :], "ctx", 1)
    tokens_f = tokens.astype(jnp.float32)
    rim_f = rim.astype(jnp.float32)
    gated = local_gate(tokens_f, rim_f, kernel).astype(jnp.bfloat16)
    stacked = lax.all_gather(
        jnp.concatenate((w_query, w_key, w_value), axis=1), "ctx", axis=0, tiled=True
    )
    full_qk = stacked[:, : 2 * qk_cols]
    full_v = stacked[:, 2 * qk_cols :]
    proj_qk = jnp.dot(gated, full_qk, preferred_element_type=jnp.float32).astype(jnp.bfloat16)
    proj_v = jnp.dot(gated, full_v, preferred_element_type=jnp.float32).astype(jnp.bfloat16)
    query_f = proj_qk[:, :qk_cols].astype(jnp.float32).reshape(length, HEADS, FEAT)
    key_f = proj_qk[:, qk_cols:].astype(jnp.float32).reshape(length, HEADS, FEAT)
    value_f = proj_v.astype(jnp.float32).reshape(length, HEADS, HEAD_DIM)
    own_state, own_norm = block_state(key_f, value_f)
    state_blocks = pack_parts(own_state, own_norm, devices)
    prefix_parts = before_sum(
        lax.all_to_all(state_blocks, "ctx", split_axis=0, concat_axis=0, tiled=True)
    )
    prefix_home = lax.all_to_all(prefix_parts, "ctx", split_axis=0, concat_axis=0, tiled=True)
    prev_state, prev_norm = unpack_parts(prefix_home, own_state, own_norm)
    out_f, back = jax.vjp(block_attend, query_f, key_f, value_f, prev_state, prev_norm)
    mixed = out_f.astype(jnp.bfloat16)
    d_query, d_key, d_value, d_state, d_norm = back(cotangent.astype(jnp.float32))
    d_query = d_query.reshape(length, qk_cols).astype(jnp.bfloat16)
    query_part = lax.dot_general(
        gated, d_query, (((0,), (0,)), ((), ())), preferred_element_type=jnp.float32
    )
    grad_blocks = pack_parts(d_state, d_norm, devices)
    query_part, grad_blocks = lax.optimization_barrier((query_part, grad_blocks))
    grad_query = lax.psum_scatter(query_part, "ctx", scatter_dimension=0, tiled=True)
    suffix_parts = after_sum(
        lax.all_to_all(grad_blocks, "ctx", split_axis=0, concat_axis=0, tiled=True)
    )
    suffix_home = lax.all_to_all(suffix_parts, "ctx", split_axis=0, concat_axis=0, tiled=True)
    later_state, later_norm = unpack_parts(suffix_home, d_state, d_norm)
    later_state, later_norm, grad_query = lax.optimization_barrier((later_state, later_norm, grad_query))
    _, back_state = jax.vjp(block_state, key_f, value_f)
    extra_key, extra_value = back_state((later_state, later_norm))
    d_key = (d_key + extra_key).reshape(length, qk_cols).astype(jnp.bfloat16)
    d_value = (d_value + extra_value).reshape(length, HEADS * HEAD_DIM).astype(jnp.bfloat16)
    d_kv = jnp.concatenate((d_key, d_value), axis=1)
    grads = lax.psum_scatter(
        lax.dot_general(gated, d_kv, (((0,), (0,)), ((), ())), preferred_element_type=jnp.float32),
        "ctx",
        scatter_dimension=0,
        tiled=True,
    )
    contract = (((1,), (1,)), ((), ()))
    d_gated = lax.dot_general(
        jnp.concatenate((d_query, d_key), axis=1), full_qk, contract, preferred_element_type=jnp.float32
    )
    d_gated = d_gated + lax.dot_general(d_value, full_v, contract, preferred_element_type=jnp.float32)
    _, back_conv = jax.vjp(local_gate, tokens_f, rim_f, kernel)
    d_tokens, d_rim, d_kernel = back_conv(d_gated)
    carried = from_behind(d_rim, "ctx", -1)
    d_tokens = jnp.concatenate((d_tokens[: length - 2], d_tokens[length - 2 :] + carried), axis=0)
    taps, width = d_kernel.shape
    d_kernel = d_kernel.reshape(taps, devices, width // devices).transpose(1, 0, 2)
    kernel_share = lax.psum_scatter(
        d_kernel.reshape(devices * taps, width // devices), "ctx", scatter_dimension=0, tiled=True
    )
    return (
        mixed,
        d_tokens.astype(jnp.bfloat16),
        grad_query,
        grads[:, :qk_cols],
        grads[:, qk_cols:],
        kernel_share,
    )


def solution(mesh):
    in_specs = (
        P(("groups", "ctx"), None),
        P(),
        P("ctx", None),
        P("ctx", None),
        P("ctx", None),
        P(("groups", "ctx"), None),
    )
    out_specs = (
        P(("groups", "ctx"), None),
        P(("groups", "ctx"), None),
        P(("groups", "ctx"), None),
        P(("groups", "ctx"), None),
        P(("groups", "ctx"), None),
        P("groups", "ctx"),
    )
    return jax.shard_map(body, mesh=mesh, in_specs=in_specs, out_specs=out_specs, check_vma=False)
```

```python
import jax
import jax.numpy as jnp
import numpy as np
from jax import lax
from jax.sharding import PartitionSpec as P

HEADS = 16
FEAT = 16
HEAD_DIM = 64


def from_behind(value, axis, steps):
    count = lax.axis_size(axis)
    first, last = (max(0, -steps), min(count, count - steps))
    return lax.ppermute(value, axis, [(source, source + steps) for source in range(first, last)])


def pair_tables(feat):
    rows, cols = np.triu_indices(feat)
    coef = np.where(rows == cols, 1.0 / np.sqrt(2.0 * feat), 1.0 / np.sqrt(1.0 * feat))
    return (rows, cols, coef)


def features(block):
    feat = block.shape[-1]
    rows, cols, coef = pair_tables(feat)
    scale = jnp.asarray(coef, jnp.float32)
    eye = np.eye(feat, dtype=np.float32)
    high = lax.Precision.HIGHEST
    pick_rows = jnp.einsum("...f,fp->...p", block, jnp.asarray(eye[:, rows]), precision=high)
    pick_cols = jnp.einsum("...f,fp->...p", block, jnp.asarray(eye[:, cols]), precision=high)
    quad = pick_rows * pick_cols * scale
    ones = jnp.ones(block.shape[:-1] + (1,), jnp.float32)
    return jnp.concatenate((ones, block * feat ** (-0.25), quad), axis=-1)


def block_attend(query, key, value, state, norm):
    length, heads, feat = query.shape
    hdim = value.shape[2]
    width = state.shape[0]
    high = lax.Precision.HIGHEST
    sigma = jnp.einsum("thf,shf->hts", query, key, precision=high) / np.sqrt(1.0 * feat)
    weight = 1.0 + sigma + 0.5 * sigma * sigma
    causal = lax.broadcasted_iota(jnp.int32, (length, length), 0) >= lax.broadcasted_iota(
        jnp.int32, (length, length), 1
    )
    weight = jnp.where(causal[None], weight, jnp.float32(0.0))
    numer = jnp.einsum("hts,she->the", weight, value, precision=high)
    denom = jnp.sum(weight, axis=2).T
    phi_query = features(query)
    numer = numer + jnp.einsum(
        "thn,nhe->the", phi_query, state.reshape(width, heads, hdim), precision=high
    )
    denom = denom + jnp.einsum("thn,nh->th", phi_query, norm, precision=high)
    attended = numer / denom[:, :, None]
    scaled = attended * lax.rsqrt(jnp.mean(attended * attended, axis=2, keepdims=True) + 1e-06)
    return scaled.reshape(length, heads * hdim)


def block_state(key, value):
    length, heads, hdim = value.shape
    phi_key = features(key)
    state = jnp.einsum("shn,she->nhe", phi_key, value, precision=lax.Precision.HIGHEST)
    return (state.reshape(phi_key.shape[2], heads * hdim), jnp.sum(phi_key, axis=0).T)


def pack_parts(state, norm, devices):
    feat, cols = state.shape
    rows = -(-feat // 40) * 40
    spare = (rows - feat) * cols
    flat = norm.reshape(-1)
    flat = jnp.concatenate((flat, jnp.zeros((spare - flat.shape[0],), jnp.float32)), axis=0)
    block = jnp.concatenate((state, flat.reshape(rows - feat, cols)), axis=0)
    row_parts = rows // 40
    col_parts = devices // row_parts
    block = block.reshape(row_parts, 40, col_parts, cols // col_parts).transpose(0, 2, 1, 3)
    return block.reshape(devices, 40, cols // col_parts)


def unpack_parts(parts, state, norm):
    feat, cols = state.shape
    devices, tall, wide = parts.shape
    col_parts = cols // wide
    row_parts = devices // col_parts
    block = parts.reshape(row_parts, col_parts, tall, wide).transpose(0, 2, 1, 3)
    block = block.reshape(row_parts * tall, cols)
    new_state = block[:feat]
    new_norm = block[feat:].reshape(-1)[: norm.size].reshape(norm.shape)
    return (new_state, new_norm)


def before_sum(block):
    zero_row = jnp.zeros((1,) + block.shape[1:], jnp.float32)
    return jnp.concatenate((zero_row, jnp.cumsum(block, axis=0)[:-1]), axis=0)


def after_sum(block):
    zero_row = jnp.zeros((1,) + block.shape[1:], jnp.float32)
    return jnp.concatenate((lax.cumsum(block[1:], axis=0, reverse=True), zero_row), axis=0)


def local_gate(tokens_f, rim_f, kernel):
    padded = jnp.concatenate((rim_f, tokens_f), axis=0)
    conv = kernel[0] * padded[2:] + kernel[1] * padded[1:-1] + kernel[2] * padded[:-2]
    return tokens_f + jax.nn.sigmoid(tokens_f) * conv


def body(tokens, kernel, w_query, w_key, w_value, cotangent):
    length = tokens.shape[0]
    qk_cols = w_query.shape[1]
    devices = lax.axis_size("ctx")
    rim = from_behind(tokens[length - 2 :], "ctx", 1)
    tokens_f = tokens.astype(jnp.float32)
    rim_f = rim.astype(jnp.float32)
    gated = local_gate(tokens_f, rim_f, kernel).astype(jnp.bfloat16)
    stacked = lax.all_gather(
        jnp.concatenate((w_query, w_key, w_value), axis=1), "ctx", axis=0, tiled=True
    )
    full_qk = stacked[:, : 2 * qk_cols]
    full_v = stacked[:, 2 * qk_cols :]
    proj_qk = jnp.dot(gated, full_qk, preferred_element_type=jnp.float32).astype(jnp.bfloat16)
    proj_v = jnp.dot(gated, full_v, preferred_element_type=jnp.float32).astype(jnp.bfloat16)
    query_f = proj_qk[:, :qk_cols].astype(jnp.float32).reshape(length, HEADS, FEAT)
    key_f = proj_qk[:, qk_cols:].astype(jnp.float32).reshape(length, HEADS, FEAT)
    value_f = proj_v.astype(jnp.float32).reshape(length, HEADS, HEAD_DIM)
    own_state, own_norm = block_state(key_f, value_f)
    state_blocks = pack_parts(own_state, own_norm, devices)
    prefix_parts = before_sum(
        lax.all_to_all(state_blocks, "ctx", split_axis=0, concat_axis=0, tiled=True)
    )
    prefix_home = lax.all_to_all(prefix_parts, "ctx", split_axis=0, concat_axis=0, tiled=True)
    prev_state, prev_norm = unpack_parts(prefix_home, own_state, own_norm)
    out_f, back = jax.vjp(block_attend, query_f, key_f, value_f, prev_state, prev_norm)
    mixed = out_f.astype(jnp.bfloat16)
    d_query, d_key, d_value, d_state, d_norm = back(cotangent.astype(jnp.float32))
    d_query = d_query.reshape(length, qk_cols).astype(jnp.bfloat16)
    query_part = lax.dot_general(
        gated, d_query, (((0,), (0,)), ((), ())), preferred_element_type=jnp.float32
    )
    grad_blocks = pack_parts(d_state, d_norm, devices)
    query_part, grad_blocks = lax.optimization_barrier((query_part, grad_blocks))
    grad_query = lax.psum_scatter(query_part, "ctx", scatter_dimension=0, tiled=True)
    suffix_parts = after_sum(
        lax.all_to_all(grad_blocks, "ctx", split_axis=0, concat_axis=0, tiled=True)
    )
    suffix_home = lax.all_to_all(suffix_parts, "ctx", split_axis=0, concat_axis=0, tiled=True)
    later_state, later_norm = unpack_parts(suffix_home, d_state, d_norm)
    _, back_state = jax.vjp(block_state, key_f, value_f)
    extra_key, extra_value = back_state((later_state, later_norm))
    d_key = (d_key + extra_key).reshape(length, qk_cols).astype(jnp.bfloat16)
    d_value = (d_value + extra_value).reshape(length, HEADS * HEAD_DIM).astype(jnp.bfloat16)
    d_kv = jnp.concatenate((d_key, d_value), axis=1)
    d_kv, grad_query = lax.optimization_barrier((d_kv, grad_query))
    grads = lax.psum_scatter(
        lax.dot_general(gated, d_kv, (((0,), (0,)), ((), ())), preferred_element_type=jnp.float32),
        "ctx",
        scatter_dimension=0,
        tiled=True,
    )
    contract = (((1,), (1,)), ((), ()))
    d_gated = lax.dot_general(
        jnp.concatenate((d_query, d_key), axis=1), full_qk, contract, preferred_element_type=jnp.float32
    )
    d_gated = d_gated + lax.dot_general(d_value, full_v, contract, preferred_element_type=jnp.float32)
    _, back_conv = jax.vjp(local_gate, tokens_f, rim_f, kernel)
    d_tokens, d_rim, d_kernel = back_conv(d_gated)
    carried = from_behind(d_rim, "ctx", -1)
    d_tokens = jnp.concatenate((d_tokens[: length - 2], d_tokens[length - 2 :] + carried), axis=0)
    taps, width = d_kernel.shape
    d_kernel = d_kernel.reshape(taps, devices, width // devices).transpose(1, 0, 2)
    kernel_share = lax.psum_scatter(
        d_kernel.reshape(devices * taps, width // devices), "ctx", scatter_dimension=0, tiled=True
    )
    return (
        mixed,
        d_tokens.astype(jnp.bfloat16),
        grad_query,
        grads[:, :qk_cols],
        grads[:, qk_cols:],
        kernel_share,
    )


def solution(mesh):
    in_specs = (
        P(("groups", "ctx"), None),
        P(),
        P("ctx", None),
        P("ctx", None),
        P("ctx", None),
        P(("groups", "ctx"), None),
    )
    out_specs = (
        P(("groups", "ctx"), None),
        P(("groups", "ctx"), None),
        P(("groups", "ctx"), None),
        P(("groups", "ctx"), None),
        P(("groups", "ctx"), None),
        P("groups", "ctx"),
    )
    return jax.shard_map(body, mesh=mesh, in_specs=in_specs, out_specs=out_specs, check_vma=False)
```

```python
import jax
import jax.numpy as jnp
import numpy as np
from jax import lax
from jax.sharding import PartitionSpec as P

HEADS = 16
FEAT = 16
HEAD_DIM = 64


def from_behind(value, axis, steps):
    count = lax.axis_size(axis)
    first, last = (max(0, -steps), min(count, count - steps))
    return lax.ppermute(value, axis, [(source, source + steps) for source in range(first, last)])


def pair_tables(feat):
    rows, cols = np.triu_indices(feat)
    coef = np.where(rows == cols, 1.0 / np.sqrt(2.0 * feat), 1.0 / np.sqrt(1.0 * feat))
    return (rows, cols, coef)


def features(block):
    feat = block.shape[-1]
    rows, cols, coef = pair_tables(feat)
    scale = jnp.asarray(coef, jnp.float32)
    eye = np.eye(feat, dtype=np.float32)
    high = lax.Precision.HIGHEST
    pick_rows = jnp.einsum("...f,fp->...p", block, jnp.asarray(eye[:, rows]), precision=high)
    pick_cols = jnp.einsum("...f,fp->...p", block, jnp.asarray(eye[:, cols]), precision=high)
    quad = pick_rows * pick_cols * scale
    ones = jnp.ones(block.shape[:-1] + (1,), jnp.float32)
    return jnp.concatenate((ones, block * feat ** (-0.25), quad), axis=-1)


def block_attend(query, key, value, state, norm):
    length, heads, feat = query.shape
    hdim = value.shape[2]
    width = state.shape[0]
    high = lax.Precision.HIGHEST
    sigma = jnp.einsum("thf,shf->hts", query, key, precision=high) / np.sqrt(1.0 * feat)
    weight = 1.0 + sigma + 0.5 * sigma * sigma
    causal = lax.broadcasted_iota(jnp.int32, (length, length), 0) >= lax.broadcasted_iota(
        jnp.int32, (length, length), 1
    )
    weight = jnp.where(causal[None], weight, jnp.float32(0.0))
    numer = jnp.einsum("hts,she->the", weight, value, precision=high)
    denom = jnp.sum(weight, axis=2).T
    phi_query = features(query)
    numer = numer + jnp.einsum(
        "thn,nhe->the", phi_query, state.reshape(width, heads, hdim), precision=high
    )
    denom = denom + jnp.einsum("thn,nh->th", phi_query, norm, precision=high)
    attended = numer / denom[:, :, None]
    scaled = attended * lax.rsqrt(jnp.mean(attended * attended, axis=2, keepdims=True) + 1e-06)
    return scaled.reshape(length, heads * hdim)


def block_state(key, value):
    length, heads, hdim = value.shape
    phi_key = features(key)
    state = jnp.einsum("shn,she->nhe", phi_key, value, precision=lax.Precision.HIGHEST)
    return (state.reshape(phi_key.shape[2], heads * hdim), jnp.sum(phi_key, axis=0).T)


def pack_parts(state, norm, devices):
    feat, cols = state.shape
    rows = -(-feat // 40) * 40
    spare = (rows - feat) * cols
    flat = norm.reshape(-1)
    flat = jnp.concatenate((flat, jnp.zeros((spare - flat.shape[0],), jnp.float32)), axis=0)
    block = jnp.concatenate((state, flat.reshape(rows - feat, cols)), axis=0)
    row_parts = rows // 40
    col_parts = devices // row_parts
    block = block.reshape(row_parts, 40, col_parts, cols // col_parts).transpose(0, 2, 1, 3)
    return block.reshape(devices, 40, cols // col_parts)


def unpack_parts(parts, state, norm):
    feat, cols = state.shape
    devices, tall, wide = parts.shape
    col_parts = cols // wide
    row_parts = devices // col_parts
    block = parts.reshape(row_parts, col_parts, tall, wide).transpose(0, 2, 1, 3)
    block = block.reshape(row_parts * tall, cols)
    new_state = block[:feat]
    new_norm = block[feat:].reshape(-1)[: norm.size].reshape(norm.shape)
    return (new_state, new_norm)


def before_sum(block):
    zero_row = jnp.zeros((1,) + block.shape[1:], jnp.float32)
    return jnp.concatenate((zero_row, jnp.cumsum(block, axis=0)[:-1]), axis=0)


def after_sum(block):
    zero_row = jnp.zeros((1,) + block.shape[1:], jnp.float32)
    return jnp.concatenate((lax.cumsum(block[1:], axis=0, reverse=True), zero_row), axis=0)


def local_gate(tokens_f, rim_f, kernel):
    padded = jnp.concatenate((rim_f, tokens_f), axis=0)
    conv = kernel[0] * padded[2:] + kernel[1] * padded[1:-1] + kernel[2] * padded[:-2]
    return tokens_f + jax.nn.sigmoid(tokens_f) * conv


def body(tokens, kernel, w_query, w_key, w_value, cotangent):
    length = tokens.shape[0]
    qk_cols = w_query.shape[1]
    devices = lax.axis_size("ctx")
    rim = from_behind(tokens[length - 2 :], "ctx", 1)
    tokens_f = tokens.astype(jnp.float32)
    rim_f = rim.astype(jnp.float32)
    gated = local_gate(tokens_f, rim_f, kernel).astype(jnp.bfloat16)
    stacked = lax.all_gather(
        jnp.concatenate((w_query, w_key, w_value), axis=1), "ctx", axis=0, tiled=True
    )
    projected = jnp.dot(gated, stacked, preferred_element_type=jnp.float32).astype(jnp.bfloat16)
    query_f = projected[:, :qk_cols].astype(jnp.float32).reshape(length, HEADS, FEAT)
    key_f = projected[:, qk_cols : 2 * qk_cols].astype(jnp.float32).reshape(length, HEADS, FEAT)
    value_f = projected[:, 2 * qk_cols :].astype(jnp.float32).reshape(length, HEADS, HEAD_DIM)
    own_state, own_norm = block_state(key_f, value_f)
    state_blocks = pack_parts(own_state, own_norm, devices)
    prefix_parts = before_sum(
        lax.all_to_all(state_blocks, "ctx", split_axis=0, concat_axis=0, tiled=True)
    )
    prefix_home = lax.all_to_all(prefix_parts, "ctx", split_axis=0, concat_axis=0, tiled=True)
    prev_state, prev_norm = unpack_parts(prefix_home, own_state, own_norm)
    out_f, back = jax.vjp(block_attend, query_f, key_f, value_f, prev_state, prev_norm)
    mixed = out_f.astype(jnp.bfloat16)
    d_query, d_key, d_value, d_state, d_norm = back(cotangent.astype(jnp.float32))
    d_query = d_query.reshape(length, qk_cols).astype(jnp.bfloat16)
    query_part = lax.dot_general(
        gated, d_query, (((0,), (0,)), ((), ())), preferred_element_type=jnp.float32
    )
    grad_blocks = pack_parts(d_state, d_norm, devices)
    query_part, grad_blocks = lax.optimization_barrier((query_part, grad_blocks))
    grad_query = lax.psum_scatter(query_part, "ctx", scatter_dimension=0, tiled=True)
    suffix_parts = after_sum(
        lax.all_to_all(grad_blocks, "ctx", split_axis=0, concat_axis=0, tiled=True)
    )
    suffix_home = lax.all_to_all(suffix_parts, "ctx", split_axis=0, concat_axis=0, tiled=True)
    later_state, later_norm = unpack_parts(suffix_home, d_state, d_norm)
    later_state, later_norm, grad_query = lax.optimization_barrier((later_state, later_norm, grad_query))
    _, back_state = jax.vjp(block_state, key_f, value_f)
    extra_key, extra_value = back_state((later_state, later_norm))
    d_key = (d_key + extra_key).reshape(length, qk_cols).astype(jnp.bfloat16)
    d_value = (d_value + extra_value).reshape(length, HEADS * HEAD_DIM).astype(jnp.bfloat16)
    d_kv = jnp.concatenate((d_key, d_value), axis=1)
    grads = lax.psum_scatter(
        lax.dot_general(gated, d_kv, (((0,), (0,)), ((), ())), preferred_element_type=jnp.float32),
        "ctx",
        scatter_dimension=0,
        tiled=True,
    )
    contract = (((1,), (1,)), ((), ()))
    d_proj = jnp.concatenate((d_query, d_kv), axis=1)
    d_gated = lax.dot_general(d_proj, stacked, contract, preferred_element_type=jnp.float32)
    _, back_conv = jax.vjp(local_gate, tokens_f, rim_f, kernel)
    d_tokens, d_rim, d_kernel = back_conv(d_gated)
    carried = from_behind(d_rim, "ctx", -1)
    d_tokens = jnp.concatenate((d_tokens[: length - 2], d_tokens[length - 2 :] + carried), axis=0)
    taps, width = d_kernel.shape
    d_kernel = d_kernel.reshape(taps, devices, width // devices).transpose(1, 0, 2)
    kernel_share = lax.psum_scatter(
        d_kernel.reshape(devices * taps, width // devices), "ctx", scatter_dimension=0, tiled=True
    )
    return (
        mixed,
        d_tokens.astype(jnp.bfloat16),
        grad_query,
        grads[:, :qk_cols],
        grads[:, qk_cols:],
        kernel_share,
    )


def solution(mesh):
    in_specs = (
        P(("groups", "ctx"), None),
        P(),
        P("ctx", None),
        P("ctx", None),
        P("ctx", None),
        P(("groups", "ctx"), None),
    )
    out_specs = (
        P(("groups", "ctx"), None),
        P(("groups", "ctx"), None),
        P(("groups", "ctx"), None),
        P(("groups", "ctx"), None),
        P(("groups", "ctx"), None),
        P("groups", "ctx"),
    )
    return jax.shard_map(body, mesh=mesh, in_specs=in_specs, out_specs=out_specs, check_vma=False)
```

```python
import jax
import jax.numpy as jnp
import numpy as np
from jax import lax
from jax.sharding import PartitionSpec as P

HEADS = 16
FEAT = 16
HEAD_DIM = 64


def from_behind(value, axis, steps):
    count = lax.axis_size(axis)
    first, last = (max(0, -steps), min(count, count - steps))
    return lax.ppermute(value, axis, [(source, source + steps) for source in range(first, last)])


def pair_tables(feat):
    rows, cols = np.triu_indices(feat)
    coef = np.where(rows == cols, 1.0 / np.sqrt(2.0 * feat), 1.0 / np.sqrt(1.0 * feat))
    return (rows, cols, coef)


def features(block):
    feat = block.shape[-1]
    rows, cols, coef = pair_tables(feat)
    scale = jnp.asarray(coef, jnp.float32)
    eye = np.eye(feat, dtype=np.float32)
    high = lax.Precision.HIGHEST
    pick_rows = jnp.einsum("...f,fp->...p", block, jnp.asarray(eye[:, rows]), precision=high)
    pick_cols = jnp.einsum("...f,fp->...p", block, jnp.asarray(eye[:, cols]), precision=high)
    quad = pick_rows * pick_cols * scale
    ones = jnp.ones(block.shape[:-1] + (1,), jnp.float32)
    return jnp.concatenate((ones, block * feat ** (-0.25), quad), axis=-1)


def block_attend(query, key, value, state, norm):
    length, heads, feat = query.shape
    hdim = value.shape[2]
    width = state.shape[0]
    high = lax.Precision.HIGHEST
    sigma = jnp.einsum("thf,shf->hts", query, key, precision=high) / np.sqrt(1.0 * feat)
    weight = 1.0 + sigma + 0.5 * sigma * sigma
    causal = lax.broadcasted_iota(jnp.int32, (length, length), 0) >= lax.broadcasted_iota(
        jnp.int32, (length, length), 1
    )
    weight = jnp.where(causal[None], weight, jnp.float32(0.0))
    numer = jnp.einsum("hts,she->the", weight, value, precision=high)
    denom = jnp.sum(weight, axis=2).T
    phi_query = features(query)
    numer = numer + jnp.einsum(
        "thn,nhe->the", phi_query, state.reshape(width, heads, hdim), precision=high
    )
    denom = denom + jnp.einsum("thn,nh->th", phi_query, norm, precision=high)
    attended = numer / denom[:, :, None]
    scaled = attended * lax.rsqrt(jnp.mean(attended * attended, axis=2, keepdims=True) + 1e-06)
    return scaled.reshape(length, heads * hdim)


def block_state(key, value):
    length, heads, hdim = value.shape
    phi_key = features(key)
    state = jnp.einsum("shn,she->nhe", phi_key, value, precision=lax.Precision.HIGHEST)
    return (state.reshape(phi_key.shape[2], heads * hdim), jnp.sum(phi_key, axis=0).T)


def pack_parts(state, norm, devices):
    feat, cols = state.shape
    rows = -(-feat // 40) * 40
    spare = (rows - feat) * cols
    flat = norm.reshape(-1)
    flat = jnp.concatenate((flat, jnp.zeros((spare - flat.shape[0],), jnp.float32)), axis=0)
    block = jnp.concatenate((state, flat.reshape(rows - feat, cols)), axis=0)
    row_parts = rows // 40
    col_parts = devices // row_parts
    block = block.reshape(row_parts, 40, col_parts, cols // col_parts).transpose(0, 2, 1, 3)
    return block.reshape(devices, 40, cols // col_parts)


def unpack_parts(parts, state, norm):
    feat, cols = state.shape
    devices, tall, wide = parts.shape
    col_parts = cols // wide
    row_parts = devices // col_parts
    block = parts.reshape(row_parts, col_parts, tall, wide).transpose(0, 2, 1, 3)
    block = block.reshape(row_parts * tall, cols)
    new_state = block[:feat]
    new_norm = block[feat:].reshape(-1)[: norm.size].reshape(norm.shape)
    return (new_state, new_norm)


def before_sum(block):
    zero_row = jnp.zeros((1,) + block.shape[1:], jnp.float32)
    return jnp.concatenate((zero_row, jnp.cumsum(block, axis=0)[:-1]), axis=0)


def after_sum(block):
    zero_row = jnp.zeros((1,) + block.shape[1:], jnp.float32)
    return jnp.concatenate((lax.cumsum(block[1:], axis=0, reverse=True), zero_row), axis=0)


def local_gate(tokens_f, rim_f, kernel):
    padded = jnp.concatenate((rim_f, tokens_f), axis=0)
    conv = kernel[0] * padded[2:] + kernel[1] * padded[1:-1] + kernel[2] * padded[:-2]
    return tokens_f + jax.nn.sigmoid(tokens_f) * conv


def body(tokens, kernel, w_query, w_key, w_value, cotangent):
    length = tokens.shape[0]
    qk_cols = w_query.shape[1]
    devices = lax.axis_size("ctx")
    rim = from_behind(tokens[length - 2 :], "ctx", 1)
    tokens_f = tokens.astype(jnp.float32)
    rim_f = rim.astype(jnp.float32)
    gated = local_gate(tokens_f, rim_f, kernel).astype(jnp.bfloat16)
    stacked = lax.all_gather(
        jnp.concatenate((w_query, w_key, w_value), axis=1), "ctx", axis=0, tiled=True
    )
    projected = jnp.dot(gated, stacked, preferred_element_type=jnp.float32).astype(jnp.bfloat16)
    query_f = projected[:, :qk_cols].astype(jnp.float32).reshape(length, HEADS, FEAT)
    key_f = projected[:, qk_cols : 2 * qk_cols].astype(jnp.float32).reshape(length, HEADS, FEAT)
    value_f = projected[:, 2 * qk_cols :].astype(jnp.float32).reshape(length, HEADS, HEAD_DIM)
    own_state, own_norm = block_state(key_f, value_f)
    state_blocks = pack_parts(own_state, own_norm, devices)
    prefix_parts = before_sum(
        lax.all_to_all(state_blocks, "ctx", split_axis=0, concat_axis=0, tiled=True)
    )
    prefix_home = lax.all_to_all(prefix_parts, "ctx", split_axis=0, concat_axis=0, tiled=True)
    prev_state, prev_norm = unpack_parts(prefix_home, own_state, own_norm)
    out_f, back = jax.vjp(block_attend, query_f, key_f, value_f, prev_state, prev_norm)
    mixed = out_f.astype(jnp.bfloat16)
    d_query, d_key, d_value, d_state, d_norm = back(cotangent.astype(jnp.float32))
    d_query = d_query.reshape(length, qk_cols).astype(jnp.bfloat16)
    query_part = lax.dot_general(
        gated, d_query, (((0,), (0,)), ((), ())), preferred_element_type=jnp.float32
    )
    grad_blocks = pack_parts(d_state, d_norm, devices)
    query_part, grad_blocks = lax.optimization_barrier((query_part, grad_blocks))
    grad_query = lax.psum_scatter(query_part, "ctx", scatter_dimension=0, tiled=True)
    suffix_parts = after_sum(
        lax.all_to_all(grad_blocks, "ctx", split_axis=0, concat_axis=0, tiled=True)
    )
    suffix_home = lax.all_to_all(suffix_parts, "ctx", split_axis=0, concat_axis=0, tiled=True)
    later_state, later_norm = unpack_parts(suffix_home, d_state, d_norm)
    later_state, later_norm, grad_query = lax.optimization_barrier((later_state, later_norm, grad_query))
    _, back_state = jax.vjp(block_state, key_f, value_f)
    extra_key, extra_value = back_state((later_state, later_norm))
    d_key = (d_key + extra_key).reshape(length, qk_cols).astype(jnp.bfloat16)
    d_value = (d_value + extra_value).reshape(length, HEADS * HEAD_DIM).astype(jnp.bfloat16)
    d_kv = jnp.concatenate((d_key, d_value), axis=1)
    outer = (((0,), (0,)), ((), ()))
    grad_key = lax.psum_scatter(
        lax.dot_general(gated, d_key, outer, preferred_element_type=jnp.float32),
        "ctx",
        scatter_dimension=0,
        tiled=True,
    )
    grad_value = lax.psum_scatter(
        lax.dot_general(gated, d_value, outer, preferred_element_type=jnp.float32),
        "ctx",
        scatter_dimension=0,
        tiled=True,
    )
    contract = (((1,), (1,)), ((), ()))
    d_proj = jnp.concatenate((d_query, d_kv), axis=1)
    d_gated = lax.dot_general(d_proj, stacked, contract, preferred_element_type=jnp.float32)
    _, back_conv = jax.vjp(local_gate, tokens_f, rim_f, kernel)
    d_tokens, d_rim, d_kernel = back_conv(d_gated)
    carried = from_behind(d_rim, "ctx", -1)
    d_tokens = jnp.concatenate((d_tokens[: length - 2], d_tokens[length - 2 :] + carried), axis=0)
    taps, width = d_kernel.shape
    d_kernel = d_kernel.reshape(taps, devices, width // devices).transpose(1, 0, 2)
    kernel_share = lax.psum_scatter(
        d_kernel.reshape(devices * taps, width // devices), "ctx", scatter_dimension=0, tiled=True
    )
    return (
        mixed,
        d_tokens.astype(jnp.bfloat16),
        grad_query,
        grad_key,
        grad_value,
        kernel_share,
    )


def solution(mesh):
    in_specs = (
        P(("groups", "ctx"), None),
        P(),
        P("ctx", None),
        P("ctx", None),
        P("ctx", None),
        P(("groups", "ctx"), None),
    )
    out_specs = (
        P(("groups", "ctx"), None),
        P(("groups", "ctx"), None),
        P(("groups", "ctx"), None),
        P(("groups", "ctx"), None),
        P(("groups", "ctx"), None),
        P("groups", "ctx"),
    )
    return jax.shard_map(body, mesh=mesh, in_specs=in_specs, out_specs=out_specs, check_vma=False)
```

```python
import jax
import jax.numpy as jnp
import numpy as np
from jax import lax
from jax.sharding import PartitionSpec as P

HEADS = 16
FEAT = 16
HEAD_DIM = 64


def from_behind(value, axis, steps):
    count = lax.axis_size(axis)
    first, last = (max(0, -steps), min(count, count - steps))
    return lax.ppermute(value, axis, [(source, source + steps) for source in range(first, last)])


def pair_tables(feat):
    rows, cols = np.triu_indices(feat)
    coef = np.where(rows == cols, 1.0 / np.sqrt(2.0 * feat), 1.0 / np.sqrt(1.0 * feat))
    return (rows, cols, coef)


def features(block):
    feat = block.shape[-1]
    rows, cols, coef = pair_tables(feat)
    scale = jnp.asarray(coef, jnp.float32)
    eye = np.eye(feat, dtype=np.float32)
    high = lax.Precision.HIGHEST
    pick_rows = jnp.einsum("...f,fp->...p", block, jnp.asarray(eye[:, rows]), precision=high)
    pick_cols = jnp.einsum("...f,fp->...p", block, jnp.asarray(eye[:, cols]), precision=high)
    quad = pick_rows * pick_cols * scale
    ones = jnp.ones(block.shape[:-1] + (1,), jnp.float32)
    return jnp.concatenate((ones, block * feat ** (-0.25), quad), axis=-1)


def block_attend(query, key, value, state, norm):
    length, heads, feat = query.shape
    hdim = value.shape[2]
    width = state.shape[0]
    high = lax.Precision.HIGHEST
    sigma = jnp.einsum("thf,shf->hts", query, key, precision=high) / np.sqrt(1.0 * feat)
    weight = 1.0 + sigma + 0.5 * sigma * sigma
    causal = lax.broadcasted_iota(jnp.int32, (length, length), 0) >= lax.broadcasted_iota(
        jnp.int32, (length, length), 1
    )
    weight = jnp.where(causal[None], weight, jnp.float32(0.0))
    numer = jnp.einsum("hts,she->the", weight, value, precision=high)
    denom = jnp.sum(weight, axis=2).T
    phi_query = features(query)
    numer = numer + jnp.einsum(
        "thn,nhe->the", phi_query, state.reshape(width, heads, hdim), precision=high
    )
    denom = denom + jnp.einsum("thn,nh->th", phi_query, norm, precision=high)
    attended = numer / denom[:, :, None]
    scaled = attended * lax.rsqrt(jnp.mean(attended * attended, axis=2, keepdims=True) + 1e-06)
    return scaled.reshape(length, heads * hdim)


def block_state(key, value):
    length, heads, hdim = value.shape
    phi_key = features(key)
    state = jnp.einsum("shn,she->nhe", phi_key, value, precision=lax.Precision.HIGHEST)
    return (state.reshape(phi_key.shape[2], heads * hdim), jnp.sum(phi_key, axis=0).T)


def pack_parts(state, norm, devices):
    feat, cols = state.shape
    rows = -(-feat // 40) * 40
    spare = (rows - feat) * cols
    flat = norm.reshape(-1)
    flat = jnp.concatenate((flat, jnp.zeros((spare - flat.shape[0],), jnp.float32)), axis=0)
    block = jnp.concatenate((state, flat.reshape(rows - feat, cols)), axis=0)
    row_parts = rows // 40
    col_parts = devices // row_parts
    block = block.reshape(row_parts, 40, col_parts, cols // col_parts).transpose(0, 2, 1, 3)
    return block.reshape(devices, 40, cols // col_parts)


def unpack_parts(parts, state, norm):
    feat, cols = state.shape
    devices, tall, wide = parts.shape
    col_parts = cols // wide
    row_parts = devices // col_parts
    block = parts.reshape(row_parts, col_parts, tall, wide).transpose(0, 2, 1, 3)
    block = block.reshape(row_parts * tall, cols)
    new_state = block[:feat]
    new_norm = block[feat:].reshape(-1)[: norm.size].reshape(norm.shape)
    return (new_state, new_norm)


def before_sum(block):
    zero_row = jnp.zeros((1,) + block.shape[1:], jnp.float32)
    return jnp.concatenate((zero_row, jnp.cumsum(block, axis=0)[:-1]), axis=0)


def after_sum(block):
    zero_row = jnp.zeros((1,) + block.shape[1:], jnp.float32)
    return jnp.concatenate((lax.cumsum(block[1:], axis=0, reverse=True), zero_row), axis=0)


def local_gate(tokens_f, rim_f, kernel):
    padded = jnp.concatenate((rim_f, tokens_f), axis=0)
    conv = kernel[0] * padded[2:] + kernel[1] * padded[1:-1] + kernel[2] * padded[:-2]
    return tokens_f + jax.nn.sigmoid(tokens_f) * conv


def body(tokens, kernel, w_query, w_key, w_value, cotangent):
    length = tokens.shape[0]
    qk_cols = w_query.shape[1]
    devices = lax.axis_size("ctx")
    rim = from_behind(tokens[length - 2 :], "ctx", 1)
    tokens_f = tokens.astype(jnp.float32)
    rim_f = rim.astype(jnp.float32)
    gated = local_gate(tokens_f, rim_f, kernel).astype(jnp.bfloat16)
    stacked = lax.all_gather(
        jnp.concatenate((w_query, w_key, w_value), axis=1), "ctx", axis=0, tiled=True
    )
    projected = jnp.dot(gated, stacked, preferred_element_type=jnp.float32).astype(jnp.bfloat16)
    query_f = projected[:, :qk_cols].astype(jnp.float32).reshape(length, HEADS, FEAT)
    key_f = projected[:, qk_cols : 2 * qk_cols].astype(jnp.float32).reshape(length, HEADS, FEAT)
    value_f = projected[:, 2 * qk_cols :].astype(jnp.float32).reshape(length, HEADS, HEAD_DIM)
    own_state, own_norm = block_state(key_f, value_f)
    state_blocks = pack_parts(own_state, own_norm, devices)
    prefix_parts = before_sum(
        lax.all_to_all(state_blocks, "ctx", split_axis=0, concat_axis=0, tiled=True)
    )
    prefix_home = lax.all_to_all(prefix_parts, "ctx", split_axis=0, concat_axis=0, tiled=True)
    prev_state, prev_norm = unpack_parts(prefix_home, own_state, own_norm)
    out_f, back = jax.vjp(block_attend, query_f, key_f, value_f, prev_state, prev_norm)
    mixed = out_f.astype(jnp.bfloat16)
    d_query, d_key, d_value, d_state, d_norm = back(cotangent.astype(jnp.float32))
    d_query = d_query.reshape(length, qk_cols).astype(jnp.bfloat16)
    grad_blocks = pack_parts(d_state, d_norm, devices)
    suffix_parts = after_sum(
        lax.all_to_all(grad_blocks, "ctx", split_axis=0, concat_axis=0, tiled=True)
    )
    suffix_home = lax.all_to_all(suffix_parts, "ctx", split_axis=0, concat_axis=0, tiled=True)
    later_state, later_norm = unpack_parts(suffix_home, d_state, d_norm)
    _, back_state = jax.vjp(block_state, key_f, value_f)
    extra_key, extra_value = back_state((later_state, later_norm))
    d_key = (d_key + extra_key).reshape(length, qk_cols).astype(jnp.bfloat16)
    d_value = (d_value + extra_value).reshape(length, HEADS * HEAD_DIM).astype(jnp.bfloat16)
    d_proj = jnp.concatenate((d_query, d_key, d_value), axis=1)
    grads = lax.psum_scatter(
        lax.dot_general(gated, d_proj, (((0,), (0,)), ((), ())), preferred_element_type=jnp.float32),
        "ctx",
        scatter_dimension=0,
        tiled=True,
    )
    contract = (((1,), (1,)), ((), ()))
    d_gated = lax.dot_general(d_proj, stacked, contract, preferred_element_type=jnp.float32)
    _, back_conv = jax.vjp(local_gate, tokens_f, rim_f, kernel)
    d_tokens, d_rim, d_kernel = back_conv(d_gated)
    carried = from_behind(d_rim, "ctx", -1)
    d_tokens = jnp.concatenate((d_tokens[: length - 2], d_tokens[length - 2 :] + carried), axis=0)
    taps, width = d_kernel.shape
    d_kernel = d_kernel.reshape(taps, devices, width // devices).transpose(1, 0, 2)
    kernel_share = lax.psum_scatter(
        d_kernel.reshape(devices * taps, width // devices), "ctx", scatter_dimension=0, tiled=True
    )
    return (
        mixed,
        d_tokens.astype(jnp.bfloat16),
        grads[:, :qk_cols],
        grads[:, qk_cols : 2 * qk_cols],
        grads[:, 2 * qk_cols :],
        kernel_share,
    )


def solution(mesh):
    in_specs = (
        P(("groups", "ctx"), None),
        P(),
        P("ctx", None),
        P("ctx", None),
        P("ctx", None),
        P(("groups", "ctx"), None),
    )
    out_specs = (
        P(("groups", "ctx"), None),
        P(("groups", "ctx"), None),
        P(("groups", "ctx"), None),
        P(("groups", "ctx"), None),
        P(("groups", "ctx"), None),
        P("groups", "ctx"),
    )
    return jax.shard_map(body, mesh=mesh, in_specs=in_specs, out_specs=out_specs, check_vma=False)
```

```python
import jax
import jax.numpy as jnp
import numpy as np
from jax import lax
from jax.sharding import PartitionSpec as P

HEADS = 16
FEAT = 16
HEAD_DIM = 64


def from_behind(value, axis, steps):
    count = lax.axis_size(axis)
    first, last = (max(0, -steps), min(count, count - steps))
    return lax.ppermute(value, axis, [(source, source + steps) for source in range(first, last)])


def pair_tables(feat):
    rows, cols = np.triu_indices(feat)
    coef = np.where(rows == cols, 1.0 / np.sqrt(2.0 * feat), 1.0 / np.sqrt(1.0 * feat))
    return (rows, cols, coef)


def features(block):
    feat = block.shape[-1]
    rows, cols, coef = pair_tables(feat)
    scale = jnp.asarray(coef, jnp.float32)
    eye = np.eye(feat, dtype=np.float32)
    high = lax.Precision.HIGHEST
    pick_rows = jnp.einsum("...f,fp->...p", block, jnp.asarray(eye[:, rows]), precision=high)
    pick_cols = jnp.einsum("...f,fp->...p", block, jnp.asarray(eye[:, cols]), precision=high)
    quad = pick_rows * pick_cols * scale
    ones = jnp.ones(block.shape[:-1] + (1,), jnp.float32)
    return jnp.concatenate((ones, block * feat ** (-0.25), quad), axis=-1)


def block_attend(query, key, value, state, norm):
    length, heads, feat = query.shape
    hdim = value.shape[2]
    width = state.shape[0]
    high = lax.Precision.HIGHEST
    sigma = jnp.einsum("thf,shf->hts", query, key, precision=high) / np.sqrt(1.0 * feat)
    weight = 1.0 + sigma + 0.5 * sigma * sigma
    causal = lax.broadcasted_iota(jnp.int32, (length, length), 0) >= lax.broadcasted_iota(
        jnp.int32, (length, length), 1
    )
    weight = jnp.where(causal[None], weight, jnp.float32(0.0))
    numer = jnp.einsum("hts,she->the", weight, value, precision=high)
    denom = jnp.sum(weight, axis=2).T
    numer, denom = lax.optimization_barrier((numer, denom))
    phi_query = features(query)
    numer = numer + jnp.einsum(
        "thn,nhe->the", phi_query, state.reshape(width, heads, hdim), precision=high
    )
    denom = denom + jnp.einsum("thn,nh->th", phi_query, norm, precision=high)
    attended = numer / denom[:, :, None]
    scaled = attended * lax.rsqrt(jnp.mean(attended * attended, axis=2, keepdims=True) + 1e-06)
    return scaled.reshape(length, heads * hdim)


def block_state(key, value):
    length, heads, hdim = value.shape
    phi_key = features(key)
    state = jnp.einsum("shn,she->nhe", phi_key, value, precision=lax.Precision.HIGHEST)
    return (state.reshape(phi_key.shape[2], heads * hdim), jnp.sum(phi_key, axis=0).T)


def pack_parts(state, norm, devices):
    feat, cols = state.shape
    rows = -(-feat // 40) * 40
    spare = (rows - feat) * cols
    flat = norm.reshape(-1)
    flat = jnp.concatenate((flat, jnp.zeros((spare - flat.shape[0],), jnp.float32)), axis=0)
    block = jnp.concatenate((state, flat.reshape(rows - feat, cols)), axis=0)
    row_parts = rows // 40
    col_parts = devices // row_parts
    block = block.reshape(row_parts, 40, col_parts, cols // col_parts).transpose(0, 2, 1, 3)
    return block.reshape(devices, 40, cols // col_parts)


def unpack_parts(parts, state, norm):
    feat, cols = state.shape
    devices, tall, wide = parts.shape
    col_parts = cols // wide
    row_parts = devices // col_parts
    block = parts.reshape(row_parts, col_parts, tall, wide).transpose(0, 2, 1, 3)
    block = block.reshape(row_parts * tall, cols)
    new_state = block[:feat]
    new_norm = block[feat:].reshape(-1)[: norm.size].reshape(norm.shape)
    return (new_state, new_norm)


def before_sum(block):
    zero_row = jnp.zeros((1,) + block.shape[1:], jnp.float32)
    return jnp.concatenate((zero_row, jnp.cumsum(block, axis=0)[:-1]), axis=0)


def after_sum(block):
    zero_row = jnp.zeros((1,) + block.shape[1:], jnp.float32)
    return jnp.concatenate((lax.cumsum(block[1:], axis=0, reverse=True), zero_row), axis=0)


def local_gate(tokens_f, rim_f, kernel):
    padded = jnp.concatenate((rim_f, tokens_f), axis=0)
    conv = kernel[0] * padded[2:] + kernel[1] * padded[1:-1] + kernel[2] * padded[:-2]
    return tokens_f + jax.nn.sigmoid(tokens_f) * conv


def body(tokens, kernel, w_query, w_key, w_value, cotangent):
    length = tokens.shape[0]
    qk_cols = w_query.shape[1]
    devices = lax.axis_size("ctx")
    rim = from_behind(tokens[length - 2 :], "ctx", 1)
    tokens_f = tokens.astype(jnp.float32)
    rim_f = rim.astype(jnp.float32)
    gated = local_gate(tokens_f, rim_f, kernel).astype(jnp.bfloat16)
    stacked = lax.all_gather(
        jnp.concatenate((w_query, w_key, w_value), axis=1), "ctx", axis=0, tiled=True
    )
    projected = jnp.dot(gated, stacked, preferred_element_type=jnp.float32).astype(jnp.bfloat16)
    query_f = projected[:, :qk_cols].astype(jnp.float32).reshape(length, HEADS, FEAT)
    key_f = projected[:, qk_cols : 2 * qk_cols].astype(jnp.float32).reshape(length, HEADS, FEAT)
    value_f = projected[:, 2 * qk_cols :].astype(jnp.float32).reshape(length, HEADS, HEAD_DIM)
    own_state, own_norm = block_state(key_f, value_f)
    state_blocks = pack_parts(own_state, own_norm, devices)
    prefix_parts = before_sum(
        lax.all_to_all(state_blocks, "ctx", split_axis=0, concat_axis=0, tiled=True)
    )
    prefix_home = lax.all_to_all(prefix_parts, "ctx", split_axis=0, concat_axis=0, tiled=True)
    prev_state, prev_norm = unpack_parts(prefix_home, own_state, own_norm)
    out_f, back = jax.vjp(block_attend, query_f, key_f, value_f, prev_state, prev_norm)
    mixed = out_f.astype(jnp.bfloat16)
    d_query, d_key, d_value, d_state, d_norm = back(cotangent.astype(jnp.float32))
    d_query = d_query.reshape(length, qk_cols).astype(jnp.bfloat16)
    grad_blocks = pack_parts(d_state, d_norm, devices)
    suffix_parts = after_sum(
        lax.all_to_all(grad_blocks, "ctx", split_axis=0, concat_axis=0, tiled=True)
    )
    suffix_home = lax.all_to_all(suffix_parts, "ctx", split_axis=0, concat_axis=0, tiled=True)
    later_state, later_norm = unpack_parts(suffix_home, d_state, d_norm)
    _, back_state = jax.vjp(block_state, key_f, value_f)
    extra_key, extra_value = back_state((later_state, later_norm))
    d_key = (d_key + extra_key).reshape(length, qk_cols).astype(jnp.bfloat16)
    d_value = (d_value + extra_value).reshape(length, HEADS * HEAD_DIM).astype(jnp.bfloat16)
    d_proj = jnp.concatenate((d_query, d_key, d_value), axis=1)
    grads = lax.psum_scatter(
        lax.dot_general(gated, d_proj, (((0,), (0,)), ((), ())), preferred_element_type=jnp.float32),
        "ctx",
        scatter_dimension=0,
        tiled=True,
    )
    contract = (((1,), (1,)), ((), ()))
    d_gated = lax.dot_general(d_proj, stacked, contract, preferred_element_type=jnp.float32)
    _, back_conv = jax.vjp(local_gate, tokens_f, rim_f, kernel)
    d_tokens, d_rim, d_kernel = back_conv(d_gated)
    carried = from_behind(d_rim, "ctx", -1)
    d_tokens = jnp.concatenate((d_tokens[: length - 2], d_tokens[length - 2 :] + carried), axis=0)
    taps, width = d_kernel.shape
    d_kernel = d_kernel.reshape(taps, devices, width // devices).transpose(1, 0, 2)
    kernel_share = lax.psum_scatter(
        d_kernel.reshape(devices * taps, width // devices), "ctx", scatter_dimension=0, tiled=True
    )
    return (
        mixed,
        d_tokens.astype(jnp.bfloat16),
        grads[:, :qk_cols],
        grads[:, qk_cols : 2 * qk_cols],
        grads[:, 2 * qk_cols :],
        kernel_share,
    )


def solution(mesh):
    in_specs = (
        P(("groups", "ctx"), None),
        P(),
        P("ctx", None),
        P("ctx", None),
        P("ctx", None),
        P(("groups", "ctx"), None),
    )
    out_specs = (
        P(("groups", "ctx"), None),
        P(("groups", "ctx"), None),
        P(("groups", "ctx"), None),
        P(("groups", "ctx"), None),
        P(("groups", "ctx"), None),
        P("groups", "ctx"),
    )
    return jax.shard_map(body, mesh=mesh, in_specs=in_specs, out_specs=out_specs, check_vma=False)
```

```python
import jax
import jax.numpy as jnp
import numpy as np
from jax import lax
from jax.sharding import PartitionSpec as P

HEADS = 16
FEAT = 16
HEAD_DIM = 64


def from_behind(value, axis, steps):
    count = lax.axis_size(axis)
    first, last = (max(0, -steps), min(count, count - steps))
    return lax.ppermute(value, axis, [(source, source + steps) for source in range(first, last)])


def pair_tables(feat):
    rows, cols = np.triu_indices(feat)
    coef = np.where(rows == cols, 1.0 / np.sqrt(2.0 * feat), 1.0 / np.sqrt(1.0 * feat))
    return (rows, cols, coef)


def features(block):
    feat = block.shape[-1]
    rows, cols, coef = pair_tables(feat)
    scale = jnp.asarray(coef, jnp.float32)
    eye = np.eye(feat, dtype=np.float32)
    high = lax.Precision.HIGHEST
    pick_rows = jnp.einsum("...f,fp->...p", block, jnp.asarray(eye[:, rows]), precision=high)
    pick_cols = jnp.einsum("...f,fp->...p", block, jnp.asarray(eye[:, cols]), precision=high)
    quad = pick_rows * pick_cols * scale
    ones = jnp.ones(block.shape[:-1] + (1,), jnp.float32)
    return jnp.concatenate((ones, block * feat ** (-0.25), quad), axis=-1)


def block_attend(query, key, value, state, norm):
    length, heads, feat = query.shape
    hdim = value.shape[2]
    width = state.shape[0]
    high = lax.Precision.HIGHEST
    sigma = jnp.einsum("thf,shf->hts", query, key, precision=high) / np.sqrt(1.0 * feat)
    weight = 1.0 + sigma + 0.5 * sigma * sigma
    causal = lax.broadcasted_iota(jnp.int32, (length, length), 0) >= lax.broadcasted_iota(
        jnp.int32, (length, length), 1
    )
    weight = jnp.where(causal[None], weight, jnp.float32(0.0))
    numer = jnp.einsum("hts,she->the", weight, value, precision=high)
    denom = jnp.sum(weight, axis=2).T
    numer, denom = lax.optimization_barrier((numer, denom))
    phi_query = features(query)
    numer = numer + jnp.einsum(
        "thn,nhe->the", phi_query, state.reshape(width, heads, hdim), precision=high
    )
    denom = denom + jnp.einsum("thn,nh->th", phi_query, norm, precision=high)
    attended = numer / denom[:, :, None]
    scaled = attended * lax.rsqrt(jnp.mean(attended * attended, axis=2, keepdims=True) + 1e-06)
    return scaled.reshape(length, heads * hdim)


def block_state(key, value):
    length, heads, hdim = value.shape
    phi_key = features(key)
    state = jnp.einsum("shn,she->nhe", phi_key, value, precision=lax.Precision.HIGHEST)
    return (state.reshape(phi_key.shape[2], heads * hdim), jnp.sum(phi_key, axis=0).T)


def pack_parts(state, norm, devices):
    feat, cols = state.shape
    rows = -(-feat // 40) * 40
    spare = (rows - feat) * cols
    flat = norm.reshape(-1)
    flat = jnp.concatenate((flat, jnp.zeros((spare - flat.shape[0],), jnp.float32)), axis=0)
    block = jnp.concatenate((state, flat.reshape(rows - feat, cols)), axis=0)
    row_parts = rows // 40
    col_parts = devices // row_parts
    block = block.reshape(row_parts, 40, col_parts, cols // col_parts).transpose(0, 2, 1, 3)
    return block.reshape(devices, 40, cols // col_parts)


def unpack_parts(parts, state, norm):
    feat, cols = state.shape
    devices, tall, wide = parts.shape
    col_parts = cols // wide
    row_parts = devices // col_parts
    block = parts.reshape(row_parts, col_parts, tall, wide).transpose(0, 2, 1, 3)
    block = block.reshape(row_parts * tall, cols)
    new_state = block[:feat]
    new_norm = block[feat:].reshape(-1)[: norm.size].reshape(norm.shape)
    return (new_state, new_norm)


def before_sum(block):
    zero_row = jnp.zeros((1,) + block.shape[1:], jnp.float32)
    return jnp.concatenate((zero_row, jnp.cumsum(block, axis=0)[:-1]), axis=0)


def after_sum(block):
    zero_row = jnp.zeros((1,) + block.shape[1:], jnp.float32)
    return jnp.concatenate((lax.cumsum(block[1:], axis=0, reverse=True), zero_row), axis=0)


def local_gate(tokens_f, rim_f, kernel):
    padded = jnp.concatenate((rim_f, tokens_f), axis=0)
    conv = kernel[0] * padded[2:] + kernel[1] * padded[1:-1] + kernel[2] * padded[:-2]
    return tokens_f + jax.nn.sigmoid(tokens_f) * conv


def body(tokens, kernel, w_query, w_key, w_value, cotangent):
    length = tokens.shape[0]
    qk_cols = w_query.shape[1]
    devices = lax.axis_size("ctx")
    rim = from_behind(tokens[length - 2 :], "ctx", 1)
    tokens_f = tokens.astype(jnp.float32)
    rim_f = rim.astype(jnp.float32)
    gated = local_gate(tokens_f, rim_f, kernel).astype(jnp.bfloat16)
    stacked = lax.all_gather(
        jnp.concatenate((w_query, w_key, w_value), axis=1), "ctx", axis=0, tiled=True
    )
    projected = jnp.dot(gated, stacked, preferred_element_type=jnp.float32).astype(jnp.bfloat16)
    query_f = projected[:, :qk_cols].astype(jnp.float32).reshape(length, HEADS, FEAT)
    key_f = projected[:, qk_cols : 2 * qk_cols].astype(jnp.float32).reshape(length, HEADS, FEAT)
    value_f = projected[:, 2 * qk_cols :].astype(jnp.float32).reshape(length, HEADS, HEAD_DIM)
    own_state, own_norm = block_state(key_f, value_f)
    state_blocks = pack_parts(own_state, own_norm, devices)
    prefix_parts = before_sum(
        lax.all_to_all(state_blocks, "ctx", split_axis=0, concat_axis=0, tiled=True)
    )
    prefix_home = lax.all_to_all(prefix_parts, "ctx", split_axis=0, concat_axis=0, tiled=True)
    prev_state, prev_norm = unpack_parts(prefix_home, own_state, own_norm)
    out_f, back = jax.vjp(block_attend, query_f, key_f, value_f, prev_state, prev_norm)
    mixed = out_f.astype(jnp.bfloat16)
    d_query, d_key, d_value, d_state, d_norm = back(cotangent.astype(jnp.float32))
    d_query = d_query.reshape(length, qk_cols).astype(jnp.bfloat16)
    outer = (((0,), (0,)), ((), ()))
    query_part = lax.dot_general(gated, d_query, outer, preferred_element_type=jnp.float32)
    grad_blocks = pack_parts(d_state, d_norm, devices)
    suffix_parts = after_sum(
        lax.all_to_all(grad_blocks, "ctx", split_axis=0, concat_axis=0, tiled=True)
    )
    suffix_home = lax.all_to_all(suffix_parts, "ctx", split_axis=0, concat_axis=0, tiled=True)
    later_state, later_norm = unpack_parts(suffix_home, d_state, d_norm)
    _, back_state = jax.vjp(block_state, key_f, value_f)
    extra_key, extra_value = back_state((later_state, later_norm))
    d_key = (d_key + extra_key).reshape(length, qk_cols).astype(jnp.bfloat16)
    d_value = (d_value + extra_value).reshape(length, HEADS * HEAD_DIM).astype(jnp.bfloat16)
    d_proj = jnp.concatenate((d_query, d_key, d_value), axis=1)
    kv_part = lax.dot_general(gated, d_proj[:, qk_cols:], outer, preferred_element_type=jnp.float32)
    grads = lax.psum_scatter(
        jnp.concatenate((query_part, kv_part), axis=1),
        "ctx",
        scatter_dimension=0,
        tiled=True,
    )
    contract = (((1,), (1,)), ((), ()))
    d_gated = lax.dot_general(d_proj, stacked, contract, preferred_element_type=jnp.float32)
    _, back_conv = jax.vjp(local_gate, tokens_f, rim_f, kernel)
    d_tokens, d_rim, d_kernel = back_conv(d_gated)
    carried = from_behind(d_rim, "ctx", -1)
    d_tokens = jnp.concatenate((d_tokens[: length - 2], d_tokens[length - 2 :] + carried), axis=0)
    taps, width = d_kernel.shape
    d_kernel = d_kernel.reshape(taps, devices, width // devices).transpose(1, 0, 2)
    kernel_share = lax.psum_scatter(
        d_kernel.reshape(devices * taps, width // devices), "ctx", scatter_dimension=0, tiled=True
    )
    return (
        mixed,
        d_tokens.astype(jnp.bfloat16),
        grads[:, :qk_cols],
        grads[:, qk_cols : 2 * qk_cols],
        grads[:, 2 * qk_cols :],
        kernel_share,
    )


def solution(mesh):
    in_specs = (
        P(("groups", "ctx"), None),
        P(),
        P("ctx", None),
        P("ctx", None),
        P("ctx", None),
        P(("groups", "ctx"), None),
    )
    out_specs = (
        P(("groups", "ctx"), None),
        P(("groups", "ctx"), None),
        P(("groups", "ctx"), None),
        P(("groups", "ctx"), None),
        P(("groups", "ctx"), None),
        P("groups", "ctx"),
    )
    return jax.shard_map(body, mesh=mesh, in_specs=in_specs, out_specs=out_specs, check_vma=False)
```
